256 devices in a mesh: spot: 16 (over x, y_hi, core), gene: 16 (over y_lo, z).
Axes of the slice: x: 4, y: 4 (y_hi: 2, y_lo: 2; y = y_hi * 2 + y_lo), z: 8, core: 2. Of those that a mesh axis runs over, the one named last changes fastest.
Arguments:
- counts: int32 [64, 512, 4096], P('spot', None, 'gene'), may hold values from 0 to 56, as said below
- tissue: int32 [64, 512], P('spot'), may hold values from 0 to 1
- tile_ids: int32 [64, 512], P('spot'), may hold values from 0 to 32767, as said below
Outputs:
- statistic: float32 [4096, 4096], P('gene', 'spot')
The draws below stay inside these ranges and needn't reach their ends.
Inputs may be any that keep to these rules, and one draw needn't show every extreme that they name: `counts`: whole numbers of molecules. `tile_ids`: bins of one tile form a rectangle of the grid; tiles are bands of rows crossed with bands of columns.
All inputs are finite; a program needn't handle non-finite values.
Results may differ from the reference program's by a relative error of at most 0.003.
Values may be sent and summed in bfloat16 or wider, within the bound.
No kernel may reach another device: no remote copies, remote signals or barrier semaphores. Data moves between devices by JAX's collectives and lax.ppermute only.
A program may use at most 64 MiB of HBM per device.

```python
import jax
import jax.numpy as jnp
from jax import lax

G = 4096
GRID_W = 512
GRID_H = 64
N_GENE = 16


def draw_counts(key, part):
    exponents = jax.random.randint(jax.random.fold_in(key, 1), (G,), 0, 4)
    levels = jnp.left_shift(jnp.ones((G,), jnp.int32), exponents.astype(jnp.int32))
    row_pos = jnp.arange(GRID_H, dtype=jnp.int32)
    row_factor = (2 * GRID_H + 6 * row_pos) // GRID_H
    upper = 1 + levels[None, None, :] * row_factor[:, None, None]
    upper = jnp.broadcast_to(upper, (GRID_H, GRID_W, G))
    drawn = jax.random.randint(jax.random.fold_in(key, 2), (GRID_H, GRID_W, G), 0, upper).astype(jnp.int32)
    return drawn.at[GRID_H - 1, 0, 0].set(56).astype(jnp.int32)


def draw_tissue(key, part):
    row_pos = jnp.arange(GRID_H, dtype=jnp.int32)
    threshold = 4 + 11 * row_pos // (GRID_H - 1)
    rolls = jax.random.randint(jax.random.fold_in(key, 21), (GRID_H, GRID_W), 0, 16).astype(jnp.int32)
    return (rolls < threshold[:, None]).astype(jnp.int32)


def draw_tile_ids(key, part):
    row_flags = (jax.random.randint(jax.random.fold_in(key, 11), (GRID_H,), 0, 12) == 0).astype(jnp.int32)
    col_flags = (jax.random.randint(jax.random.fold_in(key, 12), (GRID_W,), 0, 24) == 0).astype(jnp.int32)
    row_flags = jnp.where(jnp.arange(GRID_H, dtype=jnp.int32) == 0, 0, row_flags).astype(jnp.int32)
    col_flags = jnp.where(jnp.arange(GRID_W, dtype=jnp.int32) == 0, 0, col_flags).astype(jnp.int32)
    row_band = jnp.cumsum(row_flags).astype(jnp.int32)
    col_band = jnp.cumsum(col_flags).astype(jnp.int32)
    return (GRID_H * GRID_W - 1 - (row_band[:, None] * GRID_W + col_band[None, :])).astype(jnp.int32)


def setup_inputs(seed: int = 0) -> dict:
    arg_keys = jax.random.split(jax.random.key(seed), 4)
    return {
        "counts": draw_counts(jax.random.fold_in(arg_keys[3], 71), 0),
        "tissue": draw_tissue(jax.random.fold_in(arg_keys[3], 71), 0),
        "tile_ids": draw_tile_ids(jax.random.fold_in(arg_keys[3], 71), 0),
    }


stencil_taps = [(row_off, col_off, 1.0 / (row_off * row_off + col_off * col_off)) for row_off in range(-2, 3) for col_off in range(-2, 3) if row_off != 0 or col_off != 0]

def reference(counts, tissue, tile_ids):
    grid_rows, grid_cols, gene_total = counts.shape
    in_tissue = tissue.astype(jnp.float32)
    tissue_wide = jnp.pad(in_tissue, 2)
    ids_wide = jnp.pad(tile_ids, 2)
    weight_sq = jnp.zeros((grid_rows, grid_cols), jnp.float32)
    same_list = []
    for row_off, col_off, weight in stencil_taps:
        near_ids = ids_wide[2 + row_off:2 + row_off + grid_rows, 2 + col_off:2 + col_off + grid_cols]
        near_tissue = tissue_wide[2 + row_off:2 + row_off + grid_rows, 2 + col_off:2 + col_off + grid_cols]
        same_tile = (near_ids == tile_ids).astype(jnp.float32)
        weight_sq = weight_sq + weight * weight * same_tile * near_tissue
        same_list.append(same_tile)
    pair_norm = jnp.sum(in_tissue * weight_sq)
    tissue_count = jnp.sum(in_tissue)
    panel_width = gene_total // N_GENE

    def panel_fields(panel_index):
        values = lax.dynamic_slice_in_dim(counts, panel_index * panel_width, panel_width, 2).astype(jnp.float32)
        gene_mean = lax.optimization_barrier(jnp.sum(values * in_tissue[:, :, None], axis=(0, 1))) / tissue_count
        centred = (values - gene_mean) * in_tissue[:, :, None]
        variance = lax.optimization_barrier(jnp.sum(centred * centred, axis=(0, 1))) / tissue_count
        zscores = (centred / jnp.sqrt(variance + 1e-05)).astype(jnp.bfloat16)
        zscore_wide = jnp.pad(zscores, ((2, 2), (2, 2), (0, 0)))
        lagged_sum = jnp.zeros(values.shape, jnp.float32)
        for (row_off, col_off, weight), same_tile in zip(stencil_taps, same_list):
            near_z = zscore_wide[2 + row_off:2 + row_off + grid_rows, 2 + col_off:2 + col_off + grid_cols, :]
            lagged_sum = lagged_sum + weight * same_tile[:, :, None] * near_z.astype(jnp.float32)
        lagged = lagged_sum.astype(jnp.bfloat16)
        return (zscores.reshape(-1, panel_width), lagged.reshape(-1, panel_width))
    all_z, all_lag = lax.map(panel_fields, jnp.arange(N_GENE, dtype=jnp.int32))
    lag_cols = jnp.transpose(all_lag, (1, 0, 2)).reshape(-1, gene_total)
    contract = (((0,), (0,)), ((), ()))

    def panel_rows(z_panel):
        return lax.dot_general(z_panel, lag_cols, contract, preferred_element_type=jnp.float32)
    row_blocks = lax.map(panel_rows, all_z)
    return row_blocks.reshape(gene_total, gene_total) / jnp.sqrt(pair_norm)
```

```python
import math

import jax
import jax.numpy as jnp
from jax import lax
from jax.sharding import PartitionSpec as P

stencil_taps = [
    (row_off, col_off, 1.0 / (row_off * row_off + col_off * col_off))
    for row_off in range(-2, 3)
    for col_off in range(-2, 3)
    if row_off != 0 or col_off != 0
]
contract_bins = (((0,), (0,)), ((), ()))


def padded(cells, sides, width):
    for axis, dim in sides:
        count = lax.axis_size(axis)
        ends = count - 1
        head = lax.slice_in_dim(cells, 0, width, axis=dim)
        tail = lax.slice_in_dim(cells, cells.shape[dim] - width, cells.shape[dim], axis=dim)
        cells = jnp.concatenate(
            [
                lax.ppermute(tail, axis, [(i, (i + 1) % count) for i in range(ends)]),
                cells,
                lax.ppermute(head, axis, [((i + 1) % count, i) for i in range(ends)]),
            ],
            axis=dim,
        )
    return cells


def merge_moments(left, right):
    n_a, s_a, m_a, q_a = left
    n_b, s_b, m_b, q_b = right
    n = n_a + n_b
    gap = s_a / jnp.maximum(n_a, 1.0) - s_b / jnp.maximum(n_b, 1.0)
    m = m_a + m_b + gap * gap * (n_a * n_b / jnp.maximum(n, 1.0))
    return n, s_a + s_b, m, q_a + q_b


def allreduce_moments(moments, axis):
    count = lax.axis_size(axis)
    width = moments[1].shape[0]
    step = 1
    while step < count:
        perm = [(i, i ^ step) for i in range(count)]
        n, s, m, q = moments
        packed = jnp.concatenate([s, m, jnp.stack([n, q])])
        packed = lax.ppermute(packed, axis, perm)
        other = (packed[2 * width], packed[:width], packed[width : 2 * width], packed[2 * width + 1])
        moments = merge_moments(moments, other)
        step *= 2
    return moments


def gather_group(block, axis, members, shift):
    parts = [block]
    for t in range(1, shift):
        perm = []
        for group in members:
            size = len(group)
            for k, src in enumerate(group):
                perm.append((src, group[(k + t) % size]))
        parts.append(lax.ppermute(block, axis, perm))
    return jnp.concatenate(parts, axis=1)


def shards(counts, tissue, tile_ids):
    row_count, col_count, panel_width = counts.shape
    spot_n = lax.axis_size("spot")
    gene_n = lax.axis_size("gene")
    side = math.isqrt(gene_n)
    tile_code = tile_ids * 2 + tissue
    code_rims = padded(tile_code, (("spot", 0),), 2)
    code_wide = jnp.pad(code_rims, ((0, 0), (2, 2)))
    tissue_wide = (code_wide % 2).astype(jnp.float32)
    ids_wide = code_wide // 2
    in_tissue = tissue.astype(jnp.float32)
    weight_sq = jnp.zeros((row_count, col_count), jnp.float32)
    same_list = []
    for row_off, col_off, weight in stencil_taps:
        near_ids = ids_wide[
            2 + row_off : 2 + row_off + row_count, 2 + col_off : 2 + col_off + col_count
        ]
        near_tissue = tissue_wide[
            2 + row_off : 2 + row_off + row_count, 2 + col_off : 2 + col_off + col_count
        ]
        same_tile = (near_ids == tile_ids).astype(jnp.float32)
        weight_sq = weight_sq + weight * weight * same_tile * near_tissue
        same_list.append(same_tile)
    pair_local = jnp.sum(in_tissue * weight_sq)
    count_local = jnp.sum(in_tissue)
    values = counts.astype(jnp.float32)
    mask = in_tissue[:, :, None]
    sum_local = jnp.sum(values * mask, axis=(0, 1))
    mean_local = sum_local / jnp.maximum(count_local, 1.0)
    dev_local = (values - mean_local) * mask
    sq_local = jnp.sum(dev_local * dev_local, axis=(0, 1))
    tissue_count, total_first, sq_total, pair_norm = allreduce_moments(
        (count_local, sum_local, sq_local, pair_local), "spot"
    )
    gene_mean = total_first / tissue_count
    variance = sq_total / tissue_count
    centred = (values - gene_mean) * mask
    zscores = (centred / jnp.sqrt(variance + 1e-05)).astype(jnp.bfloat16)
    zscore_rims = padded(zscores, (("spot", 0),), 2)
    zscore_wide = jnp.pad(zscore_rims, ((0, 0), (2, 2), (0, 0)))
    lagged_sum = jnp.zeros(values.shape, jnp.float32)
    for (row_off, col_off, weight), same_tile in zip(stencil_taps, same_list):
        near_z = zscore_wide[
            2 + row_off : 2 + row_off + row_count, 2 + col_off : 2 + col_off + col_count, :
        ]
        lagged_sum = lagged_sum + weight * same_tile[:, :, None] * near_z.astype(jnp.float32)
    lagged = lagged_sum.astype(jnp.bfloat16)
    bin_count = row_count * col_count
    flat_z = zscores.reshape(bin_count, panel_width)
    flat_lag = lagged.reshape(bin_count, panel_width)
    rows = [[side * i + k for k in range(side)] for i in range(side)]
    cols = [[side * k + j for k in range(side)] for j in range(side)]
    z_cat = gather_group(flat_z, "gene", rows, side)
    lag_cat = gather_group(flat_lag, "gene", cols, side)
    block = lax.dot_general(z_cat, lag_cat, contract_bins, preferred_element_type=jnp.float32)
    block = block.reshape(side, panel_width, side, panel_width).transpose(0, 2, 1, 3)
    block = block.reshape(side * side * panel_width, panel_width)
    share = lax.psum_scatter(block, "spot", scatter_dimension=0, tiled=True)
    perm = []
    for sigma in range(spot_n):
        for c in range(gene_n):
            i, j = divmod(c, side)
            t1, t2 = divmod(sigma, side)
            g = side * i + (j - t1) % side
            s = side * ((i - t2) % side) + j
            perm.append((sigma * gene_n + c, s * gene_n + g))
    share = lax.ppermute(share, ("spot", "gene"), perm)
    return share / jnp.sqrt(pair_norm)


def solution(mesh):
    placed = (P("spot", None, "gene"), P("spot", None), P("spot", None))
    return jax.shard_map(
        shards, mesh=mesh, in_specs=placed, out_specs=P("gene", "spot"), check_vma=False
    )
```

```python
import math

import jax
import jax.numpy as jnp
from jax import lax
from jax.sharding import PartitionSpec as P

stencil_taps = [
    (row_off, col_off, 1.0 / (row_off * row_off + col_off * col_off))
    for row_off in range(-2, 3)
    for col_off in range(-2, 3)
    if row_off != 0 or col_off != 0
]
contract_bins = (((0,), (0,)), ((), ()))
GENE_AXES = ("ylo", "za", "zv")
ROW_AXES = ("ylo", "zv")
COL_AXES = ("za",)
SPOT_AXES = ("sx", "syh", "sc")
ROW_RING = [0, 1, 3, 2]
COL_RING = [0, 1, 2, 3]


def padded(cells, sides, width):
    for axis, dim in sides:
        count = lax.axis_size(axis)
        ends = count - 1
        head = lax.slice_in_dim(cells, 0, width, axis=dim)
        tail = lax.slice_in_dim(cells, cells.shape[dim] - width, cells.shape[dim], axis=dim)
        cells = jnp.concatenate(
            [
                lax.ppermute(tail, axis, [(i, (i + 1) % count) for i in range(ends)]),
                cells,
                lax.ppermute(head, axis, [((i + 1) % count, i) for i in range(ends)]),
            ],
            axis=dim,
        )
    return cells


def merge_moments(left, right):
    n_a, s_a, m_a, q_a = left
    n_b, s_b, m_b, q_b = right
    n = n_a + n_b
    gap = s_a / jnp.maximum(n_a, 1.0) - s_b / jnp.maximum(n_b, 1.0)
    m = m_a + m_b + gap * gap * (n_a * n_b / jnp.maximum(n, 1.0))
    return n, s_a + s_b, m, q_a + q_b


def allreduce_moments(moments, axis):
    count = lax.axis_size(axis)
    width = moments[1].shape[0]
    step = 1
    while step < count:
        perm = [(i, i ^ step) for i in range(count)]
        n, s, m, q = moments
        packed = jnp.concatenate([s, m, jnp.stack([n, q])])
        packed = lax.ppermute(packed, axis, perm)
        other = (packed[2 * width], packed[:width], packed[width : 2 * width], packed[2 * width + 1])
        moments = merge_moments(moments, other)
        step *= 2
    return moments


def ring_gather(block, axes, ring):
    size = len(ring)
    fwd = [(ring[k], ring[(k + 1) % size]) for k in range(size)]
    bwd = [(ring[(k + 1) % size], ring[k]) for k in range(size)]
    prev = lax.ppermute(block, axes, fwd)
    nxt = lax.ppermute(block, axes, bwd)
    half = block.shape[0] // 2
    far_lo = lax.ppermute(prev[:half], axes, fwd)
    far_hi = lax.ppermute(nxt[half:], axes, bwd)
    return [block, prev, jnp.concatenate([far_lo, far_hi], axis=0), nxt]


def unravel(index, sizes):
    out = []
    for size in reversed(sizes):
        index, rest = divmod(index, size)
        out.append(rest)
    return out[::-1]


def ravel(coords, sizes):
    index = 0
    for coord, size in zip(coords, sizes):
        index = index * size + coord
    return index


def shards(counts, tissue, tile_ids):
    row_count, col_count, panel_width = counts.shape
    spot_n = math.prod(lax.axis_size(a) for a in SPOT_AXES)
    gene_n = math.prod(lax.axis_size(a) for a in GENE_AXES)
    side = math.isqrt(gene_n)
    tile_code = tile_ids * 2 + tissue
    code_rims = padded(tile_code, ((SPOT_AXES, 0),), 2)
    code_wide = jnp.pad(code_rims, ((0, 0), (2, 2)))
    tissue_wide = (code_wide % 2).astype(jnp.float32)
    ids_wide = code_wide // 2
    in_tissue = tissue.astype(jnp.float32)
    weight_sq = jnp.zeros((row_count, col_count), jnp.float32)
    same_list = []
    for row_off, col_off, weight in stencil_taps:
        near_ids = ids_wide[
            2 + row_off : 2 + row_off + row_count, 2 + col_off : 2 + col_off + col_count
        ]
        near_tissue = tissue_wide[
            2 + row_off : 2 + row_off + row_count, 2 + col_off : 2 + col_off + col_count
        ]
        same_tile = (near_ids == tile_ids).astype(jnp.float32)
        weight_sq = weight_sq + weight * weight * same_tile * near_tissue
        same_list.append(same_tile)
    pair_local = jnp.sum(in_tissue * weight_sq)
    count_local = jnp.sum(in_tissue)
    values = counts.astype(jnp.float32)
    mask = in_tissue[:, :, None]
    sum_local = jnp.sum(values * mask, axis=(0, 1))
    mean_local = sum_local / jnp.maximum(count_local, 1.0)
    dev_local = (values - mean_local) * mask
    sq_local = jnp.sum(dev_local * dev_local, axis=(0, 1))
    tissue_count, total_first, sq_total, pair_norm = allreduce_moments(
        (count_local, sum_local, sq_local, pair_local), SPOT_AXES
    )
    gene_mean = total_first / tissue_count
    variance = sq_total / tissue_count
    centred = (values - gene_mean) * mask
    zscores = (centred / jnp.sqrt(variance + 1e-05)).astype(jnp.bfloat16)
    zscore_rims = padded(zscores, ((SPOT_AXES, 0),), 2)
    zscore_wide = jnp.pad(zscore_rims, ((0, 0), (2, 2), (0, 0)))
    lagged_sum = jnp.zeros(values.shape, jnp.float32)
    for (row_off, col_off, weight), same_tile in zip(stencil_taps, same_list):
        near_z = zscore_wide[
            2 + row_off : 2 + row_off + row_count, 2 + col_off : 2 + col_off + col_count, :
        ]
        lagged_sum = lagged_sum + weight * same_tile[:, :, None] * near_z.astype(jnp.float32)
    lagged = lagged_sum.astype(jnp.bfloat16)
    bin_count = row_count * col_count
    flat_z = zscores.reshape(bin_count, panel_width)
    flat_lag = lagged.reshape(bin_count, panel_width)
    z_parts = ring_gather(flat_z, ROW_AXES, ROW_RING)
    lag_parts = ring_gather(flat_lag, COL_AXES, COL_RING)
    z_cat = jnp.concatenate(z_parts, axis=1)
    block = jnp.concatenate(
        [lax.dot_general(z_cat, part, contract_bins, preferred_element_type=jnp.float32) for part in lag_parts],
        axis=0,
    )
    half = side * side // 2
    core = lax.axis_index("sc")
    mine = lax.dynamic_slice_in_dim(block, core * half * panel_width, half * panel_width, 0)
    other = lax.dynamic_slice_in_dim(block, (1 - core) * half * panel_width, half * panel_width, 0)
    mine = mine + lax.ppermute(other, "sc", [(0, 1), (1, 0)])
    share = lax.psum_scatter(mine, ("sx", "syh"), scatter_dimension=0, tiled=True)
    sizes = {a: lax.axis_size(a) for a in GENE_AXES}
    rings = {ROW_AXES: ROW_RING, COL_AXES: COL_RING}

    def member(coord, axes, back):
        ring = rings[axes]
        pos = ring.index(ravel([coord[a] for a in axes], [sizes[a] for a in axes]))
        out = dict(coord)
        out.update(zip(axes, unravel(ring[(pos - back) % len(ring)], [sizes[a] for a in axes])))
        return ravel([out[a] for a in GENE_AXES], [sizes[a] for a in GENE_AXES])

    perm = []
    for sigma in range(spot_n):
        q = half * (sigma % 2) + sigma // 2
        t2, t1 = divmod(q, side)
        for c in range(gene_n):
            coord = dict(zip(GENE_AXES, unravel(c, [sizes[a] for a in GENE_AXES])))
            g = member(coord, ROW_AXES, t1)
            s = member(coord, COL_AXES, t2)
            perm.append((sigma * gene_n + c, s * gene_n + g))
    share = lax.ppermute(share, SPOT_AXES + GENE_AXES, perm)
    return share / jnp.sqrt(pair_norm)


def solution(mesh):
    spot_n, gene_n = mesh.devices.shape
    y_lo = 2 if gene_n >= 16 else 1
    z_a = gene_n // (y_lo * 2)
    split = jax.sharding.Mesh(
        mesh.devices.reshape(spot_n // 4, 2, 2, y_lo, z_a, 2), SPOT_AXES + GENE_AXES
    )
    gene = GENE_AXES
    placed = (P(SPOT_AXES, None, gene), P(SPOT_AXES, None), P(SPOT_AXES, None))
    return jax.shard_map(
        shards, mesh=split, in_specs=placed, out_specs=P(gene, SPOT_AXES), check_vma=False
    )
```

```python
import math

import jax
import jax.numpy as jnp
from jax import lax
from jax.sharding import PartitionSpec as P

stencil_taps = [
    (row_off, col_off, 1.0 / (row_off * row_off + col_off * col_off))
    for row_off in range(-2, 3)
    for col_off in range(-2, 3)
    if row_off != 0 or col_off != 0
]
contract_bins = (((0,), (0,)), ((), ()))
GENE_AXES = ("ylo", "za", "zv")
ROW_AXES = ("ylo", "zv")
COL_AXES = ("za",)
SPOT_AXES = ("sx", "syh", "sc")
ROW_RING = [0, 1, 3, 2]
COL_RING = [0, 1, 2, 3]


def padded(cells, sides, width):
    for axis, dim in sides:
        count = lax.axis_size(axis)
        ends = count - 1
        head = lax.slice_in_dim(cells, 0, width, axis=dim)
        tail = lax.slice_in_dim(cells, cells.shape[dim] - width, cells.shape[dim], axis=dim)
        cells = jnp.concatenate(
            [
                lax.ppermute(tail, axis, [(i, (i + 1) % count) for i in range(ends)]),
                cells,
                lax.ppermute(head, axis, [((i + 1) % count, i) for i in range(ends)]),
            ],
            axis=dim,
        )
    return cells


def merge_moments(left, right):
    n_a, s_a, m_a, q_a = left
    n_b, s_b, m_b, q_b = right
    n = n_a + n_b
    gap = s_a / jnp.maximum(n_a, 1.0) - s_b / jnp.maximum(n_b, 1.0)
    m = m_a + m_b + gap * gap * (n_a * n_b / jnp.maximum(n, 1.0))
    return n, s_a + s_b, m, q_a + q_b


def allreduce_moments(moments, axis):
    count = lax.axis_size(axis)
    width = moments[1].shape[0]
    step = 1
    while step < count:
        perm = [(i, i ^ step) for i in range(count)]
        n, s, m, q = moments
        packed = jnp.concatenate([s, m, jnp.stack([n, q])])
        packed = lax.ppermute(packed, axis, perm)
        other = (packed[2 * width], packed[:width], packed[width : 2 * width], packed[2 * width + 1])
        moments = merge_moments(moments, other)
        step *= 2
    return moments


def ring_gather(block, axes, ring):
    size = len(ring)
    fwd = [(ring[k], ring[(k + 1) % size]) for k in range(size)]
    bwd = [(ring[(k + 1) % size], ring[k]) for k in range(size)]
    prev = lax.ppermute(block, axes, fwd)
    nxt = lax.ppermute(block, axes, bwd)
    half = block.shape[0] // 2
    far_lo = lax.ppermute(prev[:half], axes, fwd)
    far_hi = lax.ppermute(nxt[half:], axes, bwd)
    return [block, prev, jnp.concatenate([far_lo, far_hi], axis=0), nxt]


def unravel(index, sizes):
    out = []
    for size in reversed(sizes):
        index, rest = divmod(index, size)
        out.append(rest)
    return out[::-1]


def ravel(coords, sizes):
    index = 0
    for coord, size in zip(coords, sizes):
        index = index * size + coord
    return index


def shards(counts, tissue, tile_ids):
    row_count, col_count, panel_width = counts.shape
    spot_n = math.prod(lax.axis_size(a) for a in SPOT_AXES)
    gene_n = math.prod(lax.axis_size(a) for a in GENE_AXES)
    side = math.isqrt(gene_n)
    tile_code = tile_ids * 2 + tissue
    code_rims = padded(tile_code, ((SPOT_AXES, 0),), 2)
    code_wide = jnp.pad(code_rims, ((0, 0), (2, 2)))
    tissue_wide = (code_wide % 2).astype(jnp.float32)
    ids_wide = code_wide // 2
    in_tissue = tissue.astype(jnp.float32)
    weight_sq = jnp.zeros((row_count, col_count), jnp.float32)
    same_list = []
    for row_off, col_off, weight in stencil_taps:
        near_ids = ids_wide[
            2 + row_off : 2 + row_off + row_count, 2 + col_off : 2 + col_off + col_count
        ]
        near_tissue = tissue_wide[
            2 + row_off : 2 + row_off + row_count, 2 + col_off : 2 + col_off + col_count
        ]
        same_tile = (near_ids == tile_ids).astype(jnp.float32)
        weight_sq = weight_sq + weight * weight * same_tile * near_tissue
        same_list.append(same_tile)
    pair_local = jnp.sum(in_tissue * weight_sq)
    count_local = jnp.sum(in_tissue)
    values = counts.astype(jnp.float32)
    mask = in_tissue[:, :, None]
    sum_local = jnp.sum(values * mask, axis=(0, 1))
    mean_local = sum_local / jnp.maximum(count_local, 1.0)
    dev_local = (values - mean_local) * mask
    sq_local = jnp.sum(dev_local * dev_local, axis=(0, 1))
    tissue_count, total_first, sq_total, pair_norm = allreduce_moments(
        (count_local, sum_local, sq_local, pair_local), SPOT_AXES
    )
    gene_mean = total_first / tissue_count
    variance = sq_total / tissue_count
    centred = (values - gene_mean) * mask
    zscores = (centred / jnp.sqrt(variance + 1e-05)).astype(jnp.bfloat16)
    zscore_rims = padded(zscores, ((SPOT_AXES, 0),), 2)
    zscore_wide = jnp.pad(zscore_rims, ((0, 0), (2, 2), (0, 0)))
    lagged_sum = jnp.zeros(values.shape, jnp.float32)
    for (row_off, col_off, weight), same_tile in zip(stencil_taps, same_list):
        near_z = zscore_wide[
            2 + row_off : 2 + row_off + row_count, 2 + col_off : 2 + col_off + col_count, :
        ]
        lagged_sum = lagged_sum + weight * same_tile[:, :, None] * near_z.astype(jnp.float32)
    lagged = lagged_sum.astype(jnp.bfloat16)
    bin_count = row_count * col_count
    flat_z = zscores.reshape(bin_count, panel_width)
    flat_lag = lagged.reshape(bin_count, panel_width)
    z_parts = ring_gather(flat_z, ROW_AXES, ROW_RING)
    lag_parts = ring_gather(flat_lag, COL_AXES, COL_RING)
    z_cat = jnp.concatenate(z_parts, axis=1)
    block = jnp.concatenate(
        [lax.dot_general(z_cat, part, contract_bins, preferred_element_type=jnp.float32) for part in lag_parts],
        axis=0,
    )
    half = side * side // 2
    core = lax.axis_index("sc")
    mine = lax.dynamic_slice_in_dim(block, core * half * panel_width, half * panel_width, 0)
    other = lax.dynamic_slice_in_dim(block, (1 - core) * half * panel_width, half * panel_width, 0)
    mine = mine + lax.ppermute(other, "sc", [(0, 1), (1, 0)])
    ring_x = lax.axis_size("sx")
    pos_x = lax.axis_index("sx")
    pair = 2 * panel_width
    total = lax.dynamic_slice_in_dim(mine, pos_x * pair, pair, 0)
    for d in range(1, ring_x):
        sent = lax.dynamic_slice_in_dim(mine, ((pos_x + d) % ring_x) * pair, pair, 0)
        total = total + lax.ppermute(sent, "sx", [(k, (k + d) % ring_x) for k in range(ring_x)])
    high = lax.axis_index("syh")
    keep = lax.dynamic_slice_in_dim(total, high * panel_width, panel_width, 0)
    give = lax.dynamic_slice_in_dim(total, (1 - high) * panel_width, panel_width, 0)
    share = keep + lax.ppermute(give, "syh", [(0, 1), (1, 0)])
    sizes = {a: lax.axis_size(a) for a in GENE_AXES}
    rings = {ROW_AXES: ROW_RING, COL_AXES: COL_RING}

    def member(coord, axes, back):
        ring = rings[axes]
        pos = ring.index(ravel([coord[a] for a in axes], [sizes[a] for a in axes]))
        out = dict(coord)
        out.update(zip(axes, unravel(ring[(pos - back) % len(ring)], [sizes[a] for a in axes])))
        return ravel([out[a] for a in GENE_AXES], [sizes[a] for a in GENE_AXES])

    perm = []
    for sigma in range(spot_n):
        q = half * (sigma % 2) + sigma // 2
        t2, t1 = divmod(q, side)
        for c in range(gene_n):
            coord = dict(zip(GENE_AXES, unravel(c, [sizes[a] for a in GENE_AXES])))
            g = member(coord, ROW_AXES, t1)
            s = member(coord, COL_AXES, t2)
            perm.append((sigma * gene_n + c, s * gene_n + g))
    share = lax.ppermute(share, SPOT_AXES + GENE_AXES, perm)
    return share / jnp.sqrt(pair_norm)


def solution(mesh):
    spot_n, gene_n = mesh.devices.shape
    y_lo = 2 if gene_n >= 16 else 1
    z_a = gene_n // (y_lo * 2)
    split = jax.sharding.Mesh(
        mesh.devices.reshape(spot_n // 4, 2, 2, y_lo, z_a, 2), SPOT_AXES + GENE_AXES
    )
    gene = GENE_AXES
    placed = (P(SPOT_AXES, None, gene), P(SPOT_AXES, None), P(SPOT_AXES, None))
    return jax.shard_map(
        shards, mesh=split, in_specs=placed, out_specs=P(gene, SPOT_AXES), check_vma=False
    )
```

```python
import math

import jax
import jax.numpy as jnp
from jax import lax
from jax.sharding import PartitionSpec as P

stencil_taps = [
    (row_off, col_off, 1.0 / (row_off * row_off + col_off * col_off))
    for row_off in range(-2, 3)
    for col_off in range(-2, 3)
    if row_off != 0 or col_off != 0
]
contract_bins = (((0,), (0,)), ((), ()))
GENE_AXES = ("ylo", "za", "zv")
ROW_AXES = ("ylo", "zv")
COL_AXES = ("za",)
SPOT_AXES = ("sx", "syh", "sc")
ROW_RING = [0, 1, 3, 2]
COL_RING = [0, 1, 2, 3]


def padded(cells, sides, width):
    for axis, dim in sides:
        count = lax.axis_size(axis)
        ends = count - 1
        head = lax.slice_in_dim(cells, 0, width, axis=dim)
        tail = lax.slice_in_dim(cells, cells.shape[dim] - width, cells.shape[dim], axis=dim)
        cells = jnp.concatenate(
            [
                lax.ppermute(tail, axis, [(i, (i + 1) % count) for i in range(ends)]),
                cells,
                lax.ppermute(head, axis, [((i + 1) % count, i) for i in range(ends)]),
            ],
            axis=dim,
        )
    return cells


def merge_moments(left, right):
    n_a, s_a, m_a, q_a = left
    n_b, s_b, m_b, q_b = right
    n = n_a + n_b
    gap = s_a / jnp.maximum(n_a, 1.0) - s_b / jnp.maximum(n_b, 1.0)
    m = m_a + m_b + gap * gap * (n_a * n_b / jnp.maximum(n, 1.0))
    return n, s_a + s_b, m, q_a + q_b


def allreduce_moments(moments, axes):
    count = math.prod(lax.axis_size(a) for a in axes)
    width = moments[1].shape[0]
    me = lax.axis_index(axes)
    step = 1
    while step < count:
        radix = 4 if count % (step * 4) == 0 else 2
        n, s, m, q = moments
        packed = jnp.concatenate([s, m, jnp.stack([n, q])])
        got = [packed]
        for r in range(1, radix):
            perm = []
            for i in range(count):
                digit = (i // step) % radix
                perm.append((i, i + (((digit + r) % radix) - digit) * step))
            got.append(lax.ppermute(packed, axes, perm))
        digit = (me // step) % radix
        stack = jnp.stack(got)
        order = (digit - jnp.arange(radix)) % radix
        stack = jnp.take(stack, jnp.argsort(order), axis=0)
        parts = [(v[2 * width], v[:width], v[width : 2 * width], v[2 * width + 1]) for v in stack]
        while len(parts) > 1:
            parts = [merge_moments(parts[k], parts[k + 1]) for k in range(0, len(parts), 2)]
        moments = parts[0]
        step *= radix
    return moments


def ring_shift(block, axes, ring):
    size = len(ring)
    out = [block]
    for t in range(1, size):
        out.append(lax.ppermute(block, axes, [(ring[k], ring[(k + t) % size]) for k in range(size)]))
    return out


def ring_gather(block, axes, ring):
    size = len(ring)
    fwd = [(ring[k], ring[(k + 1) % size]) for k in range(size)]
    bwd = [(ring[(k + 1) % size], ring[k]) for k in range(size)]
    prev = lax.ppermute(block, axes, fwd)
    nxt = lax.ppermute(block, axes, bwd)
    half = block.shape[0] // 2
    far_lo = lax.ppermute(prev[:half], axes, fwd)
    far_hi = lax.ppermute(nxt[half:], axes, bwd)
    return [block, prev, jnp.concatenate([far_lo, far_hi], axis=0), nxt]


def unravel(index, sizes):
    out = []
    for size in reversed(sizes):
        index, rest = divmod(index, size)
        out.append(rest)
    return out[::-1]


def ravel(coords, sizes):
    index = 0
    for coord, size in zip(coords, sizes):
        index = index * size + coord
    return index


def shards(counts, tissue, tile_ids):
    row_count, col_count, panel_width = counts.shape
    spot_n = math.prod(lax.axis_size(a) for a in SPOT_AXES)
    gene_n = math.prod(lax.axis_size(a) for a in GENE_AXES)
    side = math.isqrt(gene_n)
    tile_code = tile_ids * 2 + tissue
    code_rims = padded(tile_code, ((SPOT_AXES, 0),), 2)
    code_wide = jnp.pad(code_rims, ((0, 0), (2, 2)))
    tissue_wide = (code_wide % 2).astype(jnp.float32)
    ids_wide = code_wide // 2
    in_tissue = tissue.astype(jnp.float32)
    weight_sq = jnp.zeros((row_count, col_count), jnp.float32)
    same_list = []
    for row_off, col_off, weight in stencil_taps:
        near_ids = ids_wide[
            2 + row_off : 2 + row_off + row_count, 2 + col_off : 2 + col_off + col_count
        ]
        near_tissue = tissue_wide[
            2 + row_off : 2 + row_off + row_count, 2 + col_off : 2 + col_off + col_count
        ]
        same_tile = (near_ids == tile_ids).astype(jnp.float32)
        weight_sq = weight_sq + weight * weight * same_tile * near_tissue
        same_list.append(same_tile)
    pair_local = jnp.sum(in_tissue * weight_sq)
    count_local = jnp.sum(in_tissue)
    values = counts.astype(jnp.float32)
    mask = in_tissue[:, :, None]
    bin_count = row_count * col_count
    code = jnp.where(tissue[:, :, None] > 0, counts, -1).astype(jnp.bfloat16)
    code_parts = ring_shift(code.reshape(bin_count, panel_width), ROW_AXES, ROW_RING)
    sum_local = jnp.sum(values * mask, axis=(0, 1))
    mean_local = sum_local / jnp.maximum(count_local, 1.0)
    dev_local = (values - mean_local) * mask
    sq_local = jnp.sum(dev_local * dev_local, axis=(0, 1))
    tissue_count, total_first, sq_total, pair_norm = allreduce_moments(
        (count_local, sum_local, sq_local, pair_local), SPOT_AXES
    )
    gene_mean = total_first / tissue_count
    variance = sq_total / tissue_count
    centred = (values - gene_mean) * mask
    zscores = (centred / jnp.sqrt(variance + 1e-05)).astype(jnp.bfloat16)
    stats = ring_shift(jnp.stack([gene_mean, variance]), ROW_AXES, ROW_RING)
    z_parts = [zscores.reshape(bin_count, panel_width)]
    for t in range(1, len(code_parts)):
        near = code_parts[t].astype(jnp.float32)
        near_mask = (near >= 0).astype(jnp.float32)
        near_centred = (near - stats[t][0]) * near_mask
        z_parts.append((near_centred / jnp.sqrt(stats[t][1] + 1e-05)).astype(jnp.bfloat16))
    zscore_rims = padded(zscores, ((SPOT_AXES, 0),), 2)
    zscore_wide = jnp.pad(zscore_rims, ((0, 0), (2, 2), (0, 0)))
    lagged_sum = jnp.zeros(values.shape, jnp.float32)
    for (row_off, col_off, weight), same_tile in zip(stencil_taps, same_list):
        near_z = zscore_wide[
            2 + row_off : 2 + row_off + row_count, 2 + col_off : 2 + col_off + col_count, :
        ]
        lagged_sum = lagged_sum + weight * same_tile[:, :, None] * near_z.astype(jnp.float32)
    lagged = lagged_sum.astype(jnp.bfloat16)
    flat_lag = lagged.reshape(bin_count, panel_width)
    lag_parts = ring_gather(flat_lag, COL_AXES, COL_RING)
    z_cat = jnp.concatenate(z_parts, axis=1)
    block = jnp.concatenate(
        [lax.dot_general(z_cat, part, contract_bins, preferred_element_type=jnp.float32) for part in lag_parts],
        axis=0,
    )
    half = side * side // 2
    core = lax.axis_index("sc")
    mine = lax.dynamic_slice_in_dim(block, core * half * panel_width, half * panel_width, 0)
    other = lax.dynamic_slice_in_dim(block, (1 - core) * half * panel_width, half * panel_width, 0)
    mine = mine + lax.ppermute(other, "sc", [(0, 1), (1, 0)])
    ring_x = lax.axis_size("sx")
    pos_x = lax.axis_index("sx")
    pair = 2 * panel_width
    total = lax.dynamic_slice_in_dim(mine, pos_x * pair, pair, 0)
    for d in range(1, ring_x):
        sent = lax.dynamic_slice_in_dim(mine, ((pos_x + d) % ring_x) * pair, pair, 0)
        total = total + lax.ppermute(sent, "sx", [(k, (k + d) % ring_x) for k in range(ring_x)])
    high = lax.axis_index("syh")
    keep = lax.dynamic_slice_in_dim(total, high * panel_width, panel_width, 0)
    give = lax.dynamic_slice_in_dim(total, (1 - high) * panel_width, panel_width, 0)
    share = keep + lax.ppermute(give, "syh", [(0, 1), (1, 0)])
    sizes = {a: lax.axis_size(a) for a in GENE_AXES}
    rings = {ROW_AXES: ROW_RING, COL_AXES: COL_RING}

    def member(coord, axes, back):
        ring = rings[axes]
        pos = ring.index(ravel([coord[a] for a in axes], [sizes[a] for a in axes]))
        out = dict(coord)
        out.update(zip(axes, unravel(ring[(pos - back) % len(ring)], [sizes[a] for a in axes])))
        return ravel([out[a] for a in GENE_AXES], [sizes[a] for a in GENE_AXES])

    perm = []
    for sigma in range(spot_n):
        q = half * (sigma % 2) + sigma // 2
        t2, t1 = divmod(q, side)
        for c in range(gene_n):
            coord = dict(zip(GENE_AXES, unravel(c, [sizes[a] for a in GENE_AXES])))
            g = member(coord, ROW_AXES, t1)
            s = member(coord, COL_AXES, t2)
            perm.append((sigma * gene_n + c, s * gene_n + g))
    share = lax.ppermute(share, SPOT_AXES + GENE_AXES, perm)
    return share / jnp.sqrt(pair_norm)


def solution(mesh):
    spot_n, gene_n = mesh.devices.shape
    y_lo = 2 if gene_n >= 16 else 1
    z_a = gene_n // (y_lo * 2)
    split = jax.sharding.Mesh(
        mesh.devices.reshape(spot_n // 4, 2, 2, y_lo, z_a, 2), SPOT_AXES + GENE_AXES
    )
    gene = GENE_AXES
    placed = (P(SPOT_AXES, None, gene), P(SPOT_AXES, None), P(SPOT_AXES, None))
    return jax.shard_map(
        shards, mesh=split, in_specs=placed, out_specs=P(gene, SPOT_AXES), check_vma=False
    )
```

```python
import math

import jax
import jax.numpy as jnp
from jax import lax
from jax.sharding import PartitionSpec as P

stencil_taps = [
    (row_off, col_off, 1.0 / (row_off * row_off + col_off * col_off))
    for row_off in range(-2, 3)
    for col_off in range(-2, 3)
    if row_off != 0 or col_off != 0
]
contract_bins = (((0,), (0,)), ((), ()))
GENE_AXES = ("ylo", "za", "zv")
ROW_AXES = ("ylo", "zv")
COL_AXES = ("za",)
SPOT_AXES = ("sx", "syh", "sc")
ROW_RING = [0, 1, 3, 2]
COL_RING = [0, 1, 2, 3]


def padded(cells, sides, width):
    for axis, dim in sides:
        count = lax.axis_size(axis)
        ends = count - 1
        head = lax.slice_in_dim(cells, 0, width, axis=dim)
        tail = lax.slice_in_dim(cells, cells.shape[dim] - width, cells.shape[dim], axis=dim)
        cells = jnp.concatenate(
            [
                lax.ppermute(tail, axis, [(i, (i + 1) % count) for i in range(ends)]),
                cells,
                lax.ppermute(head, axis, [((i + 1) % count, i) for i in range(ends)]),
            ],
            axis=dim,
        )
    return cells


def merge_moments(left, right):
    n_a, s_a, m_a, q_a = left
    n_b, s_b, m_b, q_b = right
    n = n_a + n_b
    gap = s_a / jnp.maximum(n_a, 1.0) - s_b / jnp.maximum(n_b, 1.0)
    m = m_a + m_b + gap * gap * (n_a * n_b / jnp.maximum(n, 1.0))
    return n, s_a + s_b, m, q_a + q_b


def allreduce_moments(moments, axes):
    count = math.prod(lax.axis_size(a) for a in axes)
    width = moments[1].shape[0]
    me = lax.axis_index(axes)
    step = 1
    while step < count:
        radix = 4 if count % (step * 4) == 0 else 2
        n, s, m, q = moments
        packed = jnp.concatenate([s, m, jnp.stack([n, q])])
        got = [packed]
        for r in range(1, radix):
            perm = []
            for i in range(count):
                digit = (i // step) % radix
                perm.append((i, i + (((digit + r) % radix) - digit) * step))
            got.append(lax.ppermute(packed, axes, perm))
        digit = (me // step) % radix
        stack = jnp.stack(got)
        order = (digit - jnp.arange(radix)) % radix
        stack = jnp.take(stack, jnp.argsort(order), axis=0)
        parts = [(v[2 * width], v[:width], v[width : 2 * width], v[2 * width + 1]) for v in stack]
        while len(parts) > 1:
            parts = [merge_moments(parts[k], parts[k + 1]) for k in range(0, len(parts), 2)]
        moments = parts[0]
        step *= radix
    return moments


def ring_gather(block, axes, ring):
    size = len(ring)
    fwd = [(ring[k], ring[(k + 1) % size]) for k in range(size)]
    bwd = [(ring[(k + 1) % size], ring[k]) for k in range(size)]
    prev = lax.ppermute(block, axes, fwd)
    nxt = lax.ppermute(block, axes, bwd)
    half = block.shape[0] // 2
    far_lo = lax.ppermute(prev[:half], axes, fwd)
    far_hi = lax.ppermute(nxt[half:], axes, bwd)
    return [block, prev, jnp.concatenate([far_lo, far_hi], axis=0), nxt]


def unravel(index, sizes):
    out = []
    for size in reversed(sizes):
        index, rest = divmod(index, size)
        out.append(rest)
    return out[::-1]


def ravel(coords, sizes):
    index = 0
    for coord, size in zip(coords, sizes):
        index = index * size + coord
    return index


def shards(counts, tissue, tile_ids):
    row_count, col_count, panel_width = counts.shape
    spot_n = math.prod(lax.axis_size(a) for a in SPOT_AXES)
    gene_n = math.prod(lax.axis_size(a) for a in GENE_AXES)
    side = math.isqrt(gene_n)
    tile_code = tile_ids * 2 + tissue
    code_rims = padded(tile_code, ((SPOT_AXES, 0),), 2)
    code_wide = jnp.pad(code_rims, ((0, 0), (2, 2)))
    tissue_wide = (code_wide % 2).astype(jnp.float32)
    ids_wide = code_wide // 2
    in_tissue = tissue.astype(jnp.float32)
    weight_sq = jnp.zeros((row_count, col_count), jnp.float32)
    same_list = []
    for row_off, col_off, weight in stencil_taps:
        near_ids = ids_wide[
            2 + row_off : 2 + row_off + row_count, 2 + col_off : 2 + col_off + col_count
        ]
        near_tissue = tissue_wide[
            2 + row_off : 2 + row_off + row_count, 2 + col_off : 2 + col_off + col_count
        ]
        same_tile = (near_ids == tile_ids).astype(jnp.float32)
        weight_sq = weight_sq + weight * weight * same_tile * near_tissue
        same_list.append(same_tile)
    pair_local = jnp.sum(in_tissue * weight_sq)
    count_local = jnp.sum(in_tissue)
    values = counts.astype(jnp.float32)
    mask = in_tissue[:, :, None]
    sum_local = jnp.sum(values * mask, axis=(0, 1))
    mean_local = sum_local / jnp.maximum(count_local, 1.0)
    dev_local = (values - mean_local) * mask
    sq_local = jnp.sum(dev_local * dev_local, axis=(0, 1))
    tissue_count, total_first, sq_total, pair_norm = allreduce_moments(
        (count_local, sum_local, sq_local, pair_local), SPOT_AXES
    )
    gene_mean = total_first / tissue_count
    variance = sq_total / tissue_count
    centred = (values - gene_mean) * mask
    zscores = (centred / jnp.sqrt(variance + 1e-05)).astype(jnp.bfloat16)
    zscore_rims = padded(zscores, ((SPOT_AXES, 0),), 2)
    zscore_wide = jnp.pad(zscore_rims, ((0, 0), (2, 2), (0, 0)))
    lagged_sum = jnp.zeros(values.shape, jnp.float32)
    for (row_off, col_off, weight), same_tile in zip(stencil_taps, same_list):
        near_z = zscore_wide[
            2 + row_off : 2 + row_off + row_count, 2 + col_off : 2 + col_off + col_count, :
        ]
        lagged_sum = lagged_sum + weight * same_tile[:, :, None] * near_z.astype(jnp.float32)
    lagged = lagged_sum.astype(jnp.bfloat16)
    bin_count = row_count * col_count
    flat_z = zscores.reshape(bin_count, panel_width)
    flat_lag = lagged.reshape(bin_count, panel_width)
    z_parts = ring_gather(flat_z, ROW_AXES, ROW_RING)
    lag_parts = ring_gather(flat_lag, COL_AXES, COL_RING)
    z_cat = jnp.concatenate(z_parts, axis=1)
    block = jnp.concatenate(
        [lax.dot_general(z_cat, part, contract_bins, preferred_element_type=jnp.float32) for part in lag_parts],
        axis=0,
    )
    half = side * side // 2
    core = lax.axis_index("sc")
    mine = lax.dynamic_slice_in_dim(block, core * half * panel_width, half * panel_width, 0)
    other = lax.dynamic_slice_in_dim(block, (1 - core) * half * panel_width, half * panel_width, 0)
    mine = mine + lax.ppermute(other, "sc", [(0, 1), (1, 0)])
    ring_x = lax.axis_size("sx")
    pos_x = lax.axis_index("sx")
    pair = 2 * panel_width
    total = lax.dynamic_slice_in_dim(mine, pos_x * pair, pair, 0)
    for d in range(1, ring_x):
        sent = lax.dynamic_slice_in_dim(mine, ((pos_x + d) % ring_x) * pair, pair, 0)
        total = total + lax.ppermute(sent, "sx", [(k, (k + d) % ring_x) for k in range(ring_x)])
    high = lax.axis_index("syh")
    keep = lax.dynamic_slice_in_dim(total, high * panel_width, panel_width, 0)
    give = lax.dynamic_slice_in_dim(total, (1 - high) * panel_width, panel_width, 0)
    share = keep + lax.ppermute(give, "syh", [(0, 1), (1, 0)])
    sizes = {a: lax.axis_size(a) for a in GENE_AXES}
    rings = {ROW_AXES: ROW_RING, COL_AXES: COL_RING}

    def member(coord, axes, back):
        ring = rings[axes]
        pos = ring.index(ravel([coord[a] for a in axes], [sizes[a] for a in axes]))
        out = dict(coord)
        out.update(zip(axes, unravel(ring[(pos - back) % len(ring)], [sizes[a] for a in axes])))
        return ravel([out[a] for a in GENE_AXES], [sizes[a] for a in GENE_AXES])

    perm = []
    for sigma in range(spot_n):
        q = half * (sigma % 2) + sigma // 2
        t2, t1 = divmod(q, side)
        for c in range(gene_n):
            coord = dict(zip(GENE_AXES, unravel(c, [sizes[a] for a in GENE_AXES])))
            g = member(coord, ROW_AXES, t1)
            s = member(coord, COL_AXES, t2)
            perm.append((sigma * gene_n + c, s * gene_n + g))
    share = lax.ppermute(share, SPOT_AXES + GENE_AXES, perm)
    return share / jnp.sqrt(pair_norm)


def solution(mesh):
    spot_n, gene_n = mesh.devices.shape
    y_lo = 2 if gene_n >= 16 else 1
    z_a = gene_n // (y_lo * 2)
    split = jax.sharding.Mesh(
        mesh.devices.reshape(spot_n // 4, 2, 2, y_lo, z_a, 2), SPOT_AXES + GENE_AXES
    )
    gene = GENE_AXES
    placed = (P(SPOT_AXES, None, gene), P(SPOT_AXES, None), P(SPOT_AXES, None))
    return jax.shard_map(
        shards, mesh=split, in_specs=placed, out_specs=P(gene, SPOT_AXES), check_vma=False
    )
```

```python
import math

import jax
import jax.numpy as jnp
from jax import lax
from jax.sharding import PartitionSpec as P

stencil_taps = [
    (row_off, col_off, 1.0 / (row_off * row_off + col_off * col_off))
    for row_off in range(-2, 3)
    for col_off in range(-2, 3)
    if row_off != 0 or col_off != 0
]
contract_bins = (((0,), (0,)), ((), ()))
GENE_AXES = ("ylo", "za", "zv")
ROW_AXES = ("ylo", "zv")
COL_AXES = ("za",)
SPOT_AXES = ("sx", "syh", "sc")
ROW_RING = [0, 1, 3, 2]
COL_RING = [0, 1, 2, 3]


def padded(cells, sides, width):
    for axis, dim in sides:
        count = lax.axis_size(axis)
        ends = count - 1
        head = lax.slice_in_dim(cells, 0, width, axis=dim)
        tail = lax.slice_in_dim(cells, cells.shape[dim] - width, cells.shape[dim], axis=dim)
        cells = jnp.concatenate(
            [
                lax.ppermute(tail, axis, [(i, (i + 1) % count) for i in range(ends)]),
                cells,
                lax.ppermute(head, axis, [((i + 1) % count, i) for i in range(ends)]),
            ],
            axis=dim,
        )
    return cells


def merge_moments(left, right):
    n_a, s_a, m_a, q_a = left
    n_b, s_b, m_b, q_b = right
    n = n_a + n_b
    gap = s_a / jnp.maximum(n_a, 1.0) - s_b / jnp.maximum(n_b, 1.0)
    m = m_a + m_b + gap * gap * (n_a * n_b / jnp.maximum(n, 1.0))
    return n, s_a + s_b, m, q_a + q_b


def allreduce_moments(moments, axis):
    count = lax.axis_size(axis)
    width = moments[1].shape[0]
    step = 1
    while step < count:
        perm = [(i, i ^ step) for i in range(count)]
        n, s, m, q = moments
        packed = jnp.concatenate([s, m, jnp.stack([n, q])])
        packed = lax.ppermute(packed, axis, perm)
        other = (packed[2 * width], packed[:width], packed[width : 2 * width], packed[2 * width + 1])
        moments = merge_moments(moments, other)
        step *= 2
    return moments


def ring_gather(block, axes, ring):
    size = len(ring)
    fwd = [(ring[k], ring[(k + 1) % size]) for k in range(size)]
    bwd = [(ring[(k + 1) % size], ring[k]) for k in range(size)]
    prev = lax.ppermute(block, axes, fwd)
    nxt = lax.ppermute(block, axes, bwd)
    half = block.shape[0] // 2
    far_lo = lax.ppermute(prev[:half], axes, fwd)
    far_hi = lax.ppermute(nxt[half:], axes, bwd)
    return [block, prev, jnp.concatenate([far_lo, far_hi], axis=0), nxt]


def unravel(index, sizes):
    out = []
    for size in reversed(sizes):
        index, rest = divmod(index, size)
        out.append(rest)
    return out[::-1]


def ravel(coords, sizes):
    index = 0
    for coord, size in zip(coords, sizes):
        index = index * size + coord
    return index


def shards(counts, tissue, tile_ids):
    row_count, col_count, panel_width = counts.shape
    spot_n = math.prod(lax.axis_size(a) for a in SPOT_AXES)
    gene_n = math.prod(lax.axis_size(a) for a in GENE_AXES)
    side = math.isqrt(gene_n)
    tile_code = tile_ids * 2 + tissue
    code_rims = padded(tile_code, ((SPOT_AXES, 0),), 2)
    code_wide = jnp.pad(code_rims, ((0, 0), (2, 2)))
    tissue_wide = (code_wide % 2).astype(jnp.float32)
    ids_wide = code_wide // 2
    in_tissue = tissue.astype(jnp.float32)
    weight_sq = jnp.zeros((row_count, col_count), jnp.float32)
    same_list = []
    for row_off, col_off, weight in stencil_taps:
        near_ids = ids_wide[
            2 + row_off : 2 + row_off + row_count, 2 + col_off : 2 + col_off + col_count
        ]
        near_tissue = tissue_wide[
            2 + row_off : 2 + row_off + row_count, 2 + col_off : 2 + col_off + col_count
        ]
        same_tile = (near_ids == tile_ids).astype(jnp.float32)
        weight_sq = weight_sq + weight * weight * same_tile * near_tissue
        same_list.append(same_tile)
    pair_local = jnp.sum(in_tissue * weight_sq)
    count_local = jnp.sum(in_tissue)
    values = counts.astype(jnp.float32)
    mask = in_tissue[:, :, None]
    sum_local = jnp.sum(values * mask, axis=(0, 1))
    mean_local = sum_local / jnp.maximum(count_local, 1.0)
    dev_local = (values - mean_local) * mask
    sq_local = jnp.sum(dev_local * dev_local, axis=(0, 1))
    tissue_count, total_first, sq_total, pair_norm = allreduce_moments(
        (count_local, sum_local, sq_local, pair_local), SPOT_AXES
    )
    gene_mean = total_first / tissue_count
    variance = sq_total / tissue_count
    centred = (values - gene_mean) * mask
    zscores = (centred / jnp.sqrt(variance + 1e-05)).astype(jnp.bfloat16)
    zscore_rims = padded(zscores, ((SPOT_AXES, 0),), 2)
    zscore_wide = jnp.pad(zscore_rims, ((0, 0), (2, 2), (0, 0)))
    lagged_sum = jnp.zeros(values.shape, jnp.float32)
    for (row_off, col_off, weight), same_tile in zip(stencil_taps, same_list):
        near_z = zscore_wide[
            2 + row_off : 2 + row_off + row_count, 2 + col_off : 2 + col_off + col_count, :
        ]
        lagged_sum = lagged_sum + weight * same_tile[:, :, None] * near_z.astype(jnp.float32)
    lagged = lagged_sum.astype(jnp.bfloat16)
    bin_count = row_count * col_count
    flat_z = zscores.reshape(bin_count, panel_width)
    flat_lag = lagged.reshape(bin_count, panel_width)
    z_parts = ring_gather(flat_z, ROW_AXES, ROW_RING)
    lag_parts = ring_gather(flat_lag, COL_AXES, COL_RING)
    z_cat = jnp.concatenate(z_parts, axis=1)
    block = jnp.concatenate(
        [lax.dot_general(z_cat, part, contract_bins, preferred_element_type=jnp.float32) for part in lag_parts],
        axis=0,
    )
    half = side * side // 2
    core = lax.axis_index("sc")
    mine = lax.dynamic_slice_in_dim(block, core * half * panel_width, half * panel_width, 0)
    other = lax.dynamic_slice_in_dim(block, (1 - core) * half * panel_width, half * panel_width, 0)
    mine = mine + lax.ppermute(other, "sc", [(0, 1), (1, 0)])
    ring_x = lax.axis_size("sx")
    pos_x = lax.axis_index("sx")
    pair = 2 * panel_width
    total = lax.dynamic_slice_in_dim(mine, pos_x * pair, pair, 0)
    for d in range(1, ring_x):
        sent = lax.dynamic_slice_in_dim(mine, ((pos_x + d) % ring_x) * pair, pair, 0)
        total = total + lax.ppermute(sent, "sx", [(k, (k + d) % ring_x) for k in range(ring_x)])
    high = lax.axis_index("syh")
    keep = lax.dynamic_slice_in_dim(total, high * panel_width, panel_width, 0)
    give = lax.dynamic_slice_in_dim(total, (1 - high) * panel_width, panel_width, 0)
    sizes = {a: lax.axis_size(a) for a in GENE_AXES}
    rings = {ROW_AXES: ROW_RING, COL_AXES: COL_RING}

    def member(coord, axes, back):
        ring = rings[axes]
        pos = ring.index(ravel([coord[a] for a in axes], [sizes[a] for a in axes]))
        out = dict(coord)
        out.update(zip(axes, unravel(ring[(pos - back) % len(ring)], [sizes[a] for a in axes])))
        return ravel([out[a] for a in GENE_AXES], [sizes[a] for a in GENE_AXES])

    def home(sigma, c):
        q = half * (sigma % 2) + sigma // 2
        t2, t1 = divmod(q, side)
        coord = dict(zip(GENE_AXES, unravel(c, [sizes[a] for a in GENE_AXES])))
        g = member(coord, ROW_AXES, t1)
        s = member(coord, COL_AXES, t2)
        return s * gene_n + g

    keep_perm, give_perm = [], []
    for sigma in range(spot_n):
        for c in range(gene_n):
            keep_perm.append((sigma * gene_n + c, home(sigma, c)))
            give_perm.append((sigma * gene_n + c, home(sigma ^ 2, c)))
    every = SPOT_AXES + GENE_AXES
    share = lax.ppermute(keep, every, keep_perm) + lax.ppermute(give, every, give_perm)
    return share / jnp.sqrt(pair_norm)


def solution(mesh):
    spot_n, gene_n = mesh.devices.shape
    y_lo = 2 if gene_n >= 16 else 1
    z_a = gene_n // (y_lo * 2)
    split = jax.sharding.Mesh(
        mesh.devices.reshape(spot_n // 4, 2, 2, y_lo, z_a, 2), SPOT_AXES + GENE_AXES
    )
    gene = GENE_AXES
    placed = (P(SPOT_AXES, None, gene), P(SPOT_AXES, None), P(SPOT_AXES, None))
    return jax.shard_map(
        shards, mesh=split, in_specs=placed, out_specs=P(gene, SPOT_AXES), check_vma=False
    )
```

```python
import math

import jax
import jax.numpy as jnp
from jax import lax
from jax.sharding import PartitionSpec as P

stencil_taps = [
    (row_off, col_off, 1.0 / (row_off * row_off + col_off * col_off))
    for row_off in range(-2, 3)
    for col_off in range(-2, 3)
    if row_off != 0 or col_off != 0
]
contract_bins = (((0,), (0,)), ((), ()))
GENE_AXES = ("ylo", "za", "zv")
ROW_AXES = ("ylo", "zv")
COL_AXES = ("za",)
SPOT_AXES = ("sx", "syh", "sc")
ROW_RING = [0, 1, 3, 2]
COL_RING = [0, 1, 2, 3]


def padded(cells, sides, width):
    for axis, dim in sides:
        count = lax.axis_size(axis)
        ends = count - 1
        head = lax.slice_in_dim(cells, 0, width, axis=dim)
        tail = lax.slice_in_dim(cells, cells.shape[dim] - width, cells.shape[dim], axis=dim)
        cells = jnp.concatenate(
            [
                lax.ppermute(tail, axis, [(i, (i + 1) % count) for i in range(ends)]),
                cells,
                lax.ppermute(head, axis, [((i + 1) % count, i) for i in range(ends)]),
            ],
            axis=dim,
        )
    return cells


def merge_moments(left, right):
    n_a, s_a, m_a, q_a = left
    n_b, s_b, m_b, q_b = right
    n = n_a + n_b
    gap = s_a / jnp.maximum(n_a, 1.0) - s_b / jnp.maximum(n_b, 1.0)
    m = m_a + m_b + gap * gap * (n_a * n_b / jnp.maximum(n, 1.0))
    return n, s_a + s_b, m, q_a + q_b


def allreduce_moments(moments, axis):
    count = lax.axis_size(axis)
    width = moments[1].shape[0]
    step = 1
    while step < count:
        perm = [(i, i ^ step) for i in range(count)]
        n, s, m, q = moments
        packed = jnp.concatenate([s, m, jnp.stack([n, q])])
        packed = lax.ppermute(packed, axis, perm)
        other = (packed[2 * width], packed[:width], packed[width : 2 * width], packed[2 * width + 1])
        moments = merge_moments(moments, other)
        step *= 2
    return moments


def ring_gather(block, axes, ring):
    size = len(ring)
    fwd = [(ring[k], ring[(k + 1) % size]) for k in range(size)]
    bwd = [(ring[(k + 1) % size], ring[k]) for k in range(size)]
    prev = lax.ppermute(block, axes, fwd)
    nxt = lax.ppermute(block, axes, bwd)
    half = block.shape[0] // 2
    far_lo = lax.ppermute(prev[:half], axes, fwd)
    far_hi = lax.ppermute(nxt[half:], axes, bwd)
    return [block, prev, jnp.concatenate([far_lo, far_hi], axis=0), nxt]


def unravel(index, sizes):
    out = []
    for size in reversed(sizes):
        index, rest = divmod(index, size)
        out.append(rest)
    return out[::-1]


def ravel(coords, sizes):
    index = 0
    for coord, size in zip(coords, sizes):
        index = index * size + coord
    return index


def shards(counts, tissue, tile_ids):
    row_count, col_count, panel_width = counts.shape
    spot_n = math.prod(lax.axis_size(a) for a in SPOT_AXES)
    gene_n = math.prod(lax.axis_size(a) for a in GENE_AXES)
    side = math.isqrt(gene_n)
    tile_code = tile_ids * 2 + tissue
    code_rims = padded(tile_code, ((SPOT_AXES, 0),), 2)
    code_wide = jnp.pad(code_rims, ((0, 0), (2, 2)))
    tissue_wide = (code_wide % 2).astype(jnp.float32)
    ids_wide = code_wide // 2
    in_tissue = tissue.astype(jnp.float32)
    weight_sq = jnp.zeros((row_count, col_count), jnp.float32)
    same_list = []
    for row_off, col_off, weight in stencil_taps:
        near_ids = ids_wide[
            2 + row_off : 2 + row_off + row_count, 2 + col_off : 2 + col_off + col_count
        ]
        near_tissue = tissue_wide[
            2 + row_off : 2 + row_off + row_count, 2 + col_off : 2 + col_off + col_count
        ]
        same_tile = (near_ids == tile_ids).astype(jnp.float32)
        weight_sq = weight_sq + weight * weight * same_tile * near_tissue
        same_list.append(same_tile)
    pair_local = jnp.sum(in_tissue * weight_sq)
    count_local = jnp.sum(in_tissue)
    values = counts.astype(jnp.float32)
    mask = in_tissue[:, :, None]
    sum_local = jnp.sum(values * mask, axis=(0, 1))
    mean_local = sum_local / jnp.maximum(count_local, 1.0)
    dev_local = (values - mean_local) * mask
    sq_local = jnp.sum(dev_local * dev_local, axis=(0, 1))
    tissue_count, total_first, sq_total, pair_norm = allreduce_moments(
        (count_local, sum_local, sq_local, pair_local), SPOT_AXES
    )
    gene_mean = total_first / tissue_count
    variance = sq_total / tissue_count
    centred = (values - gene_mean) * mask
    zscores = (centred / jnp.sqrt(variance + 1e-05)).astype(jnp.bfloat16)
    zscore_rims = padded(zscores, ((SPOT_AXES, 0),), 2)
    zscore_wide = jnp.pad(zscore_rims, ((0, 0), (2, 2), (0, 0)))
    lagged_sum = jnp.zeros(values.shape, jnp.float32)
    for (row_off, col_off, weight), same_tile in zip(stencil_taps, same_list):
        near_z = zscore_wide[
            2 + row_off : 2 + row_off + row_count, 2 + col_off : 2 + col_off + col_count, :
        ]
        lagged_sum = lagged_sum + weight * same_tile[:, :, None] * near_z.astype(jnp.float32)
    lagged = lagged_sum.astype(jnp.bfloat16)
    bin_count = row_count * col_count
    flat_z = zscores.reshape(bin_count, panel_width)
    flat_lag = lagged.reshape(bin_count, panel_width)
    z_parts = ring_gather(flat_z, COL_AXES, COL_RING)
    lag_parts = ring_gather(flat_lag, ROW_AXES, ROW_RING)
    z_cat = jnp.concatenate(z_parts, axis=1)
    block = jnp.concatenate(
        [lax.dot_general(z_cat, part, contract_bins, preferred_element_type=jnp.float32) for part in lag_parts],
        axis=0,
    )
    half = side * side // 2
    core = lax.axis_index("sc")
    mine = lax.dynamic_slice_in_dim(block, core * half * panel_width, half * panel_width, 0)
    other = lax.dynamic_slice_in_dim(block, (1 - core) * half * panel_width, half * panel_width, 0)
    mine = mine + lax.ppermute(other, "sc", [(0, 1), (1, 0)])
    ring_x = lax.axis_size("sx")
    pos_x = lax.axis_index("sx")
    pair = 2 * panel_width
    total = lax.dynamic_slice_in_dim(mine, pos_x * pair, pair, 0)
    for d in range(1, ring_x):
        sent = lax.dynamic_slice_in_dim(mine, ((pos_x + d) % ring_x) * pair, pair, 0)
        total = total + lax.ppermute(sent, "sx", [(k, (k + d) % ring_x) for k in range(ring_x)])
    high = lax.axis_index("syh")
    keep = lax.dynamic_slice_in_dim(total, high * panel_width, panel_width, 0)
    give = lax.dynamic_slice_in_dim(total, (1 - high) * panel_width, panel_width, 0)
    sizes = {a: lax.axis_size(a) for a in GENE_AXES}
    rings = {ROW_AXES: ROW_RING, COL_AXES: COL_RING}

    def member(coord, axes, back):
        ring = rings[axes]
        pos = ring.index(ravel([coord[a] for a in axes], [sizes[a] for a in axes]))
        out = dict(coord)
        out.update(zip(axes, unravel(ring[(pos - back) % len(ring)], [sizes[a] for a in axes])))
        return ravel([out[a] for a in GENE_AXES], [sizes[a] for a in GENE_AXES])

    def home(sigma, c):
        q = half * (sigma % 2) + sigma // 2
        t2, t1 = divmod(q, side)
        coord = dict(zip(GENE_AXES, unravel(c, [sizes[a] for a in GENE_AXES])))
        g = member(coord, COL_AXES, t1)
        s = member(coord, ROW_AXES, t2)
        return s * gene_n + g

    keep_perm, give_perm = [], []
    for sigma in range(spot_n):
        for c in range(gene_n):
            keep_perm.append((sigma * gene_n + c, home(sigma, c)))
            give_perm.append((sigma * gene_n + c, home(sigma ^ 2, c)))
    every = SPOT_AXES + GENE_AXES
    share = lax.ppermute(keep, every, keep_perm) + lax.ppermute(give, every, give_perm)
    return share / jnp.sqrt(pair_norm)


def solution(mesh):
    spot_n, gene_n = mesh.devices.shape
    y_lo = 2 if gene_n >= 16 else 1
    z_a = gene_n // (y_lo * 2)
    split = jax.sharding.Mesh(
        mesh.devices.reshape(spot_n // 4, 2, 2, y_lo, z_a, 2), SPOT_AXES + GENE_AXES
    )
    gene = GENE_AXES
    placed = (P(SPOT_AXES, None, gene), P(SPOT_AXES, None), P(SPOT_AXES, None))
    return jax.shard_map(
        shards, mesh=split, in_specs=placed, out_specs=P(gene, SPOT_AXES), check_vma=False
    )
```

```python
import math

import jax
import jax.numpy as jnp
from jax import lax
from jax.sharding import PartitionSpec as P

stencil_taps = [
    (row_off, col_off, 1.0 / (row_off * row_off + col_off * col_off))
    for row_off in range(-2, 3)
    for col_off in range(-2, 3)
    if row_off != 0 or col_off != 0
]
contract_bins = (((0,), (0,)), ((), ()))
GENE_AXES = ("ylo", "za", "zv")
ROW_AXES = ("ylo", "zv")
COL_AXES = ("za",)
SPOT_AXES = ("sx", "syh", "sc")
ROW_RING = [0, 1, 3, 2]
COL_RING = [0, 1, 2, 3]


def padded(cells, sides, width):
    for axis, dim in sides:
        count = lax.axis_size(axis)
        ends = count - 1
        head = lax.slice_in_dim(cells, 0, width, axis=dim)
        tail = lax.slice_in_dim(cells, cells.shape[dim] - width, cells.shape[dim], axis=dim)
        cells = jnp.concatenate(
            [
                lax.ppermute(tail, axis, [(i, (i + 1) % count) for i in range(ends)]),
                cells,
                lax.ppermute(head, axis, [((i + 1) % count, i) for i in range(ends)]),
            ],
            axis=dim,
        )
    return cells


def allreduce_sum(vector, axes):
    count = math.prod(lax.axis_size(a) for a in axes)
    step = 1
    while step < count:
        vector = vector + lax.ppermute(vector, axes, [(i, i ^ step) for i in range(count)])
        step *= 2
    return vector


def centred_square_sum(n, s1, s2):
    base = 1 << 14
    s2_hi, s2_lo = s2 >> 14, s2 & (base - 1)
    s1_hi, s1_lo = s1 >> 14, s1 & (base - 1)
    c0 = n * s2_lo - s1_lo * s1_lo
    c1 = n * s2_hi - 2 * s1_hi * s1_lo + (c0 >> 14)
    c2 = -s1_hi * s1_hi + (c1 >> 14)
    upper = (c2 * base + (c1 & (base - 1))).astype(jnp.float32)
    return upper * base + (c0 & (base - 1)).astype(jnp.float32)


def ring_gather(block, axes, ring):
    size = len(ring)
    fwd = [(ring[k], ring[(k + 1) % size]) for k in range(size)]
    bwd = [(ring[(k + 1) % size], ring[k]) for k in range(size)]
    prev = lax.ppermute(block, axes, fwd)
    nxt = lax.ppermute(block, axes, bwd)
    half = block.shape[0] // 2
    far_lo = lax.ppermute(prev[:half], axes, fwd)
    far_hi = lax.ppermute(nxt[half:], axes, bwd)
    return [block, prev, jnp.concatenate([far_lo, far_hi], axis=0), nxt]


def unravel(index, sizes):
    out = []
    for size in reversed(sizes):
        index, rest = divmod(index, size)
        out.append(rest)
    return out[::-1]


def ravel(coords, sizes):
    index = 0
    for coord, size in zip(coords, sizes):
        index = index * size + coord
    return index


def shards(counts, tissue, tile_ids):
    row_count, col_count, panel_width = counts.shape
    spot_n = math.prod(lax.axis_size(a) for a in SPOT_AXES)
    gene_n = math.prod(lax.axis_size(a) for a in GENE_AXES)
    side = math.isqrt(gene_n)
    tile_code = tile_ids * 2 + tissue
    code_rims = padded(tile_code, ((SPOT_AXES, 0),), 2)
    code_wide = jnp.pad(code_rims, ((0, 0), (2, 2)))
    tissue_wide = code_wide % 2
    ids_wide = code_wide // 2
    weight_sq = jnp.zeros((row_count, col_count), jnp.int32)
    same_list = []
    for row_off, col_off, weight in stencil_taps:
        near_ids = ids_wide[
            2 + row_off : 2 + row_off + row_count, 2 + col_off : 2 + col_off + col_count
        ]
        near_tissue = tissue_wide[
            2 + row_off : 2 + row_off + row_count, 2 + col_off : 2 + col_off + col_count
        ]
        same = near_ids == tile_ids
        scaled = round(1600 * weight * weight)
        weight_sq = weight_sq + jnp.where(same, near_tissue * scaled, 0)
        same_list.append(same.astype(jnp.float32))
    in_tissue = tissue.astype(jnp.float32)
    mask = in_tissue[:, :, None]
    inside = jnp.where(tissue[:, :, None] > 0, counts, 0)
    local = jnp.concatenate(
        [
            jnp.sum(inside, axis=(0, 1)),
            jnp.sum(inside * inside, axis=(0, 1)),
            jnp.stack([jnp.sum(tissue), jnp.sum(tissue * weight_sq)]),
        ]
    )
    total = allreduce_sum(local, SPOT_AXES)
    count_int = total[2 * panel_width]
    tissue_count = count_int.astype(jnp.float32)
    pair_norm = total[2 * panel_width + 1].astype(jnp.float32) / 1600.0
    gene_mean = total[:panel_width].astype(jnp.float32) / tissue_count
    variance = (
        centred_square_sum(count_int, total[:panel_width], total[panel_width : 2 * panel_width])
        / tissue_count
        / tissue_count
    )
    values = counts.astype(jnp.float32)
    centred = (values - gene_mean) * mask
    zscores = (centred / jnp.sqrt(variance + 1e-05)).astype(jnp.bfloat16)
    zscore_rims = padded(zscores, ((SPOT_AXES, 0),), 2)
    zscore_wide = jnp.pad(zscore_rims, ((0, 0), (2, 2), (0, 0)))
    lagged_sum = jnp.zeros(values.shape, jnp.float32)
    for (row_off, col_off, weight), same_tile in zip(stencil_taps, same_list):
        near_z = zscore_wide[
            2 + row_off : 2 + row_off + row_count, 2 + col_off : 2 + col_off + col_count, :
        ]
        lagged_sum = lagged_sum + weight * same_tile[:, :, None] * near_z.astype(jnp.float32)
    lagged = lagged_sum.astype(jnp.bfloat16)
    bin_count = row_count * col_count
    flat_z = zscores.reshape(bin_count, panel_width)
    flat_lag = lagged.reshape(bin_count, panel_width)
    z_parts = ring_gather(flat_z, ROW_AXES, ROW_RING)
    lag_parts = ring_gather(flat_lag, COL_AXES, COL_RING)
    z_cat = jnp.concatenate(z_parts, axis=1)
    block = jnp.concatenate(
        [lax.dot_general(z_cat, part, contract_bins, preferred_element_type=jnp.float32) for part in lag_parts],
        axis=0,
    )
    half = side * side // 2
    core = lax.axis_index("sc")
    mine = lax.dynamic_slice_in_dim(block, core * half * panel_width, half * panel_width, 0)
    other = lax.dynamic_slice_in_dim(block, (1 - core) * half * panel_width, half * panel_width, 0)
    mine = mine + lax.ppermute(other, "sc", [(0, 1), (1, 0)])
    ring_x = lax.axis_size("sx")
    pos_x = lax.axis_index("sx")
    pair = 2 * panel_width
    total = lax.dynamic_slice_in_dim(mine, pos_x * pair, pair, 0)
    for d in range(1, ring_x):
        sent = lax.dynamic_slice_in_dim(mine, ((pos_x + d) % ring_x) * pair, pair, 0)
        total = total + lax.ppermute(sent, "sx", [(k, (k + d) % ring_x) for k in range(ring_x)])
    high = lax.axis_index("syh")
    keep = lax.dynamic_slice_in_dim(total, high * panel_width, panel_width, 0)
    give = lax.dynamic_slice_in_dim(total, (1 - high) * panel_width, panel_width, 0)
    sizes = {a: lax.axis_size(a) for a in GENE_AXES}
    rings = {ROW_AXES: ROW_RING, COL_AXES: COL_RING}

    def member(coord, axes, back):
        ring = rings[axes]
        pos = ring.index(ravel([coord[a] for a in axes], [sizes[a] for a in axes]))
        out = dict(coord)
        out.update(zip(axes, unravel(ring[(pos - back) % len(ring)], [sizes[a] for a in axes])))
        return ravel([out[a] for a in GENE_AXES], [sizes[a] for a in GENE_AXES])

    def home(sigma, c):
        q = half * (sigma % 2) + sigma // 2
        t2, t1 = divmod(q, side)
        coord = dict(zip(GENE_AXES, unravel(c, [sizes[a] for a in GENE_AXES])))
        g = member(coord, ROW_AXES, t1)
        s = member(coord, COL_AXES, t2)
        return s * gene_n + g

    keep_perm, give_perm = [], []
    for sigma in range(spot_n):
        for c in range(gene_n):
            keep_perm.append((sigma * gene_n + c, home(sigma, c)))
            give_perm.append((sigma * gene_n + c, home(sigma ^ 2, c)))
    every = SPOT_AXES + GENE_AXES
    share = lax.ppermute(keep, every, keep_perm) + lax.ppermute(give, every, give_perm)
    return share / jnp.sqrt(pair_norm)


def solution(mesh):
    spot_n, gene_n = mesh.devices.shape
    y_lo = 2 if gene_n >= 16 else 1
    z_a = gene_n // (y_lo * 2)
    split = jax.sharding.Mesh(
        mesh.devices.reshape(spot_n // 4, 2, 2, y_lo, z_a, 2), SPOT_AXES + GENE_AXES
    )
    gene = GENE_AXES
    placed = (P(SPOT_AXES, None, gene), P(SPOT_AXES, None), P(SPOT_AXES, None))
    return jax.shard_map(
        shards, mesh=split, in_specs=placed, out_specs=P(gene, SPOT_AXES), check_vma=False
    )
```

```python
import math

import jax
import jax.numpy as jnp
from jax import lax
from jax.sharding import PartitionSpec as P

stencil_taps = [
    (row_off, col_off, 1.0 / (row_off * row_off + col_off * col_off))
    for row_off in range(-2, 3)
    for col_off in range(-2, 3)
    if row_off != 0 or col_off != 0
]
contract_bins = (((0,), (0,)), ((), ()))
GENE_AXES = ("ylo", "za", "zv")
ROW_AXES = ("ylo", "zv")
COL_AXES = ("za",)
SPOT_AXES = ("sx", "syh", "sc")
ROW_RING = [0, 1, 3, 2]
COL_RING = [0, 1, 2, 3]


def padded(cells, sides, width):
    for axis, dim in sides:
        count = lax.axis_size(axis)
        ends = count - 1
        head = lax.slice_in_dim(cells, 0, width, axis=dim)
        tail = lax.slice_in_dim(cells, cells.shape[dim] - width, cells.shape[dim], axis=dim)
        cells = jnp.concatenate(
            [
                lax.ppermute(tail, axis, [(i, (i + 1) % count) for i in range(ends)]),
                cells,
                lax.ppermute(head, axis, [((i + 1) % count, i) for i in range(ends)]),
            ],
            axis=dim,
        )
    return cells


def allreduce_sum(vector, axes):
    count = math.prod(lax.axis_size(a) for a in axes)
    step = 1
    while step < count:
        vector = vector + lax.ppermute(vector, axes, [(i, i ^ step) for i in range(count)])
        step *= 2
    return vector


def centred_square_sum(n, s1, s2):
    base = 1 << 14
    s2_hi, s2_lo = s2 >> 14, s2 & (base - 1)
    s1_hi, s1_lo = s1 >> 14, s1 & (base - 1)
    c0 = n * s2_lo - s1_lo * s1_lo
    c1 = n * s2_hi - 2 * s1_hi * s1_lo + (c0 >> 14)
    c2 = -s1_hi * s1_hi + (c1 >> 14)
    upper = (c2 * base + (c1 & (base - 1))).astype(jnp.float32)
    return upper * base + (c0 & (base - 1)).astype(jnp.float32)


def ring_gather(block, axes, ring):
    size = len(ring)
    fwd = [(ring[k], ring[(k + 1) % size]) for k in range(size)]
    bwd = [(ring[(k + 1) % size], ring[k]) for k in range(size)]
    prev = lax.ppermute(block, axes, fwd)
    nxt = lax.ppermute(block, axes, bwd)
    half = block.shape[0] // 2
    far_lo = lax.ppermute(prev[:half], axes, fwd)
    far_hi = lax.ppermute(nxt[half:], axes, bwd)
    return [block, prev, jnp.concatenate([far_lo, far_hi], axis=0), nxt]


def unravel(index, sizes):
    out = []
    for size in reversed(sizes):
        index, rest = divmod(index, size)
        out.append(rest)
    return out[::-1]


def ravel(coords, sizes):
    index = 0
    for coord, size in zip(coords, sizes):
        index = index * size + coord
    return index


def shards(counts, tissue, tile_ids):
    row_count, col_count, panel_width = counts.shape
    spot_n = math.prod(lax.axis_size(a) for a in SPOT_AXES)
    gene_n = math.prod(lax.axis_size(a) for a in GENE_AXES)
    side = math.isqrt(gene_n)
    tile_code = tile_ids * 2 + tissue
    code_rims = padded(tile_code, ((SPOT_AXES, 0),), 2)
    code_wide = jnp.pad(code_rims, ((0, 0), (2, 2)))
    tissue_wide = code_wide % 2
    ids_wide = code_wide // 2
    weight_sq = jnp.zeros((row_count, col_count), jnp.int32)
    same_list = []
    for row_off, col_off, weight in stencil_taps:
        near_ids = ids_wide[
            2 + row_off : 2 + row_off + row_count, 2 + col_off : 2 + col_off + col_count
        ]
        near_tissue = tissue_wide[
            2 + row_off : 2 + row_off + row_count, 2 + col_off : 2 + col_off + col_count
        ]
        same = near_ids == tile_ids
        scaled = round(1600 * weight * weight)
        weight_sq = weight_sq + jnp.where(same, near_tissue * scaled, 0)
        same_list.append(same.astype(jnp.float32))
    in_tissue = tissue.astype(jnp.float32)
    mask = in_tissue[:, :, None]
    inside = jnp.where(tissue[:, :, None] > 0, counts, 0)
    local = jnp.concatenate(
        [
            jnp.sum(inside, axis=(0, 1)),
            jnp.sum(inside * inside, axis=(0, 1)),
            jnp.stack([jnp.sum(tissue), jnp.sum(tissue * weight_sq)]),
        ]
    )
    total = allreduce_sum(local, SPOT_AXES)
    count_int = total[2 * panel_width]
    tissue_count = count_int.astype(jnp.float32)
    pair_norm = total[2 * panel_width + 1].astype(jnp.float32) / 1600.0
    gene_mean = total[:panel_width].astype(jnp.float32) / tissue_count
    variance = (
        centred_square_sum(count_int, total[:panel_width], total[panel_width : 2 * panel_width])
        / tissue_count
        / tissue_count
    )
    values = counts.astype(jnp.float32)
    centred = (values - gene_mean) * mask
    zscores = (centred / jnp.sqrt(variance + 1e-05)).astype(jnp.bfloat16)
    zscore_rims = padded(zscores, ((SPOT_AXES, 0),), 2)
    zscore_wide = jnp.pad(zscore_rims, ((0, 0), (2, 2), (0, 0)))
    lagged_sum = jnp.zeros(values.shape, jnp.float32)
    for (row_off, col_off, weight), same_tile in zip(stencil_taps, same_list):
        near_z = zscore_wide[
            2 + row_off : 2 + row_off + row_count, 2 + col_off : 2 + col_off + col_count, :
        ]
        lagged_sum = lagged_sum + weight * same_tile[:, :, None] * near_z.astype(jnp.float32)
    lagged = lagged_sum.astype(jnp.bfloat16)
    bin_count = row_count * col_count
    flat_z = zscores.reshape(bin_count, panel_width)
    flat_lag = lagged.reshape(bin_count, panel_width)
    z_parts = ring_gather(flat_z, ROW_AXES, ROW_RING)
    lag_parts = ring_gather(flat_lag, COL_AXES, COL_RING)
    z_cat = jnp.concatenate(z_parts, axis=1)
    block = jnp.concatenate(
        [lax.dot_general(z_cat, part, contract_bins, preferred_element_type=jnp.float32) for part in lag_parts],
        axis=0,
    )
    half = side * side // 2
    core = lax.axis_index("sc")
    mine = lax.dynamic_slice_in_dim(block, core * half * panel_width, half * panel_width, 0)
    other = lax.dynamic_slice_in_dim(block, (1 - core) * half * panel_width, half * panel_width, 0)
    mine = mine + lax.ppermute(other, "sc", [(0, 1), (1, 0)])
    ring_x = lax.axis_size("sx")
    pos_x = lax.axis_index("sx")
    pair = 2 * panel_width
    def part(d):
        return lax.dynamic_slice_in_dim(mine, ((pos_x + d) % ring_x) * pair, pair, 0)

    up = [(k, (k + 1) % ring_x) for k in range(ring_x)]
    down = [((k + 1) % ring_x, k) for k in range(ring_x)]
    if ring_x == 4:
        far = part(2)
        got_up = lax.ppermute(jnp.concatenate([part(1), far[:panel_width]]), "sx", up)
        got_down = lax.ppermute(jnp.concatenate([part(3), far[panel_width:]]), "sx", down)
        relay_lo = lax.ppermute(got_up[pair:], "sx", up)
        relay_hi = lax.ppermute(got_down[pair:], "sx", down)
        total = part(0) + got_up[:pair] + got_down[:pair] + jnp.concatenate([relay_lo, relay_hi])
    else:
        total = part(0)
        for d in range(1, ring_x):
            total = total + lax.ppermute(part(d), "sx", [(k, (k + d) % ring_x) for k in range(ring_x)])
    high = lax.axis_index("syh")
    keep = lax.dynamic_slice_in_dim(total, high * panel_width, panel_width, 0)
    give = lax.dynamic_slice_in_dim(total, (1 - high) * panel_width, panel_width, 0)
    sizes = {a: lax.axis_size(a) for a in GENE_AXES}
    rings = {ROW_AXES: ROW_RING, COL_AXES: COL_RING}

    def member(coord, axes, back):
        ring = rings[axes]
        pos = ring.index(ravel([coord[a] for a in axes], [sizes[a] for a in axes]))
        out = dict(coord)
        out.update(zip(axes, unravel(ring[(pos - back) % len(ring)], [sizes[a] for a in axes])))
        return ravel([out[a] for a in GENE_AXES], [sizes[a] for a in GENE_AXES])

    def home(sigma, c):
        q = half * (sigma % 2) + sigma // 2
        t2, t1 = divmod(q, side)
        coord = dict(zip(GENE_AXES, unravel(c, [sizes[a] for a in GENE_AXES])))
        g = member(coord, ROW_AXES, t1)
        s = member(coord, COL_AXES, t2)
        return s * gene_n + g

    keep_perm, give_perm = [], []
    for sigma in range(spot_n):
        for c in range(gene_n):
            keep_perm.append((sigma * gene_n + c, home(sigma, c)))
            give_perm.append((sigma * gene_n + c, home(sigma ^ 2, c)))
    every = SPOT_AXES + GENE_AXES
    share = lax.ppermute(keep, every, keep_perm) + lax.ppermute(give, every, give_perm)
    return share / jnp.sqrt(pair_norm)


def solution(mesh):
    spot_n, gene_n = mesh.devices.shape
    y_lo = 2 if gene_n >= 16 else 1
    z_a = gene_n // (y_lo * 2)
    split = jax.sharding.Mesh(
        mesh.devices.reshape(spot_n // 4, 2, 2, y_lo, z_a, 2), SPOT_AXES + GENE_AXES
    )
    gene = GENE_AXES
    placed = (P(SPOT_AXES, None, gene), P(SPOT_AXES, None), P(SPOT_AXES, None))
    return jax.shard_map(
        shards, mesh=split, in_specs=placed, out_specs=P(gene, SPOT_AXES), check_vma=False
    )
```

```python
import math

import jax
import jax.numpy as jnp
from jax import lax
from jax.sharding import PartitionSpec as P

stencil_taps = [
    (row_off, col_off, 1.0 / (row_off * row_off + col_off * col_off))
    for row_off in range(-2, 3)
    for col_off in range(-2, 3)
    if row_off != 0 or col_off != 0
]
contract_bins = (((0,), (0,)), ((), ()))
GENE_AXES = ("ylo", "za", "zv")
ROW_AXES = ("ylo", "zv")
COL_AXES = ("za",)
SPOT_AXES = ("sx", "syh", "sc")
ROW_RING = [0, 1, 3, 2]
COL_RING = [0, 1, 2, 3]


def padded(cells, sides, width):
    for axis, dim in sides:
        count = lax.axis_size(axis)
        ends = count - 1
        head = lax.slice_in_dim(cells, 0, width, axis=dim)
        tail = lax.slice_in_dim(cells, cells.shape[dim] - width, cells.shape[dim], axis=dim)
        cells = jnp.concatenate(
            [
                lax.ppermute(tail, axis, [(i, (i + 1) % count) for i in range(ends)]),
                cells,
                lax.ppermute(head, axis, [((i + 1) % count, i) for i in range(ends)]),
            ],
            axis=dim,
        )
    return cells


def allreduce_sum(vector, axes):
    count = math.prod(lax.axis_size(a) for a in axes)
    step = 1
    while step < count:
        vector = vector + lax.ppermute(vector, axes, [(i, i ^ step) for i in range(count)])
        step *= 2
    return vector


def centred_square_sum(n, s1, s2):
    base = 1 << 14
    s2_hi, s2_lo = s2 >> 14, s2 & (base - 1)
    s1_hi, s1_lo = s1 >> 14, s1 & (base - 1)
    c0 = n * s2_lo - s1_lo * s1_lo
    c1 = n * s2_hi - 2 * s1_hi * s1_lo + (c0 >> 14)
    c2 = -s1_hi * s1_hi + (c1 >> 14)
    upper = (c2 * base + (c1 & (base - 1))).astype(jnp.float32)
    return upper * base + (c0 & (base - 1)).astype(jnp.float32)


def ring_gather(block, axes, ring):
    size = len(ring)
    fwd = [(ring[k], ring[(k + 1) % size]) for k in range(size)]
    bwd = [(ring[(k + 1) % size], ring[k]) for k in range(size)]
    prev = lax.ppermute(block, axes, fwd)
    nxt = lax.ppermute(block, axes, bwd)
    half = block.shape[0] // 2
    far_lo = lax.ppermute(prev[:half], axes, fwd)
    far_hi = lax.ppermute(nxt[half:], axes, bwd)
    return [block, prev, jnp.concatenate([far_lo, far_hi], axis=0), nxt]


def unravel(index, sizes):
    out = []
    for size in reversed(sizes):
        index, rest = divmod(index, size)
        out.append(rest)
    return out[::-1]


def ravel(coords, sizes):
    index = 0
    for coord, size in zip(coords, sizes):
        index = index * size + coord
    return index


def shards(counts, tissue, tile_ids):
    row_count, col_count, panel_width = counts.shape
    spot_n = math.prod(lax.axis_size(a) for a in SPOT_AXES)
    gene_n = math.prod(lax.axis_size(a) for a in GENE_AXES)
    side = math.isqrt(gene_n)
    tile_code = tile_ids * 2 + tissue
    code_rims = padded(tile_code, ((SPOT_AXES, 0),), 2)
    code_wide = jnp.pad(code_rims, ((0, 0), (2, 2)))
    tissue_wide = code_wide % 2
    ids_wide = code_wide // 2
    weight_sq = jnp.zeros((row_count, col_count), jnp.int32)
    same_list = []
    for row_off, col_off, weight in stencil_taps:
        near_ids = ids_wide[
            2 + row_off : 2 + row_off + row_count, 2 + col_off : 2 + col_off + col_count
        ]
        near_tissue = tissue_wide[
            2 + row_off : 2 + row_off + row_count, 2 + col_off : 2 + col_off + col_count
        ]
        same = near_ids == tile_ids
        scaled = round(1600 * weight * weight)
        weight_sq = weight_sq + jnp.where(same, near_tissue * scaled, 0)
        same_list.append(same.astype(jnp.float32))
    in_tissue = tissue.astype(jnp.float32)
    mask = in_tissue[:, :, None]
    inside = jnp.where(tissue[:, :, None] > 0, counts, 0)
    local = jnp.concatenate(
        [
            jnp.sum(inside, axis=(0, 1)),
            jnp.sum(inside * inside, axis=(0, 1)),
            jnp.stack([jnp.sum(tissue), jnp.sum(tissue * weight_sq)]),
        ]
    )
    total = allreduce_sum(local, SPOT_AXES)
    count_int = total[2 * panel_width]
    tissue_count = count_int.astype(jnp.float32)
    pair_norm = total[2 * panel_width + 1].astype(jnp.float32) / 1600.0
    gene_mean = total[:panel_width].astype(jnp.float32) / tissue_count
    variance = (
        centred_square_sum(count_int, total[:panel_width], total[panel_width : 2 * panel_width])
        / tissue_count
        / tissue_count
    )
    values = counts.astype(jnp.float32)
    centred = (values - gene_mean) * mask
    zscores = (centred / jnp.sqrt(variance + 1e-05)).astype(jnp.bfloat16)
    zscore_rims = padded(zscores, ((SPOT_AXES, 0),), 2)
    zscore_wide = jnp.pad(zscore_rims, ((0, 0), (2, 2), (0, 0)))
    lagged_sum = jnp.zeros(values.shape, jnp.float32)
    for (row_off, col_off, weight), same_tile in zip(stencil_taps, same_list):
        near_z = zscore_wide[
            2 + row_off : 2 + row_off + row_count, 2 + col_off : 2 + col_off + col_count, :
        ]
        lagged_sum = lagged_sum + weight * same_tile[:, :, None] * near_z.astype(jnp.float32)
    lagged = lagged_sum.astype(jnp.bfloat16)
    bin_count = row_count * col_count
    flat_z = zscores.reshape(bin_count, panel_width)
    flat_lag = lagged.reshape(bin_count, panel_width)
    z_parts = ring_gather(flat_z, ROW_AXES, ROW_RING)
    lag_parts = ring_gather(flat_lag, COL_AXES, COL_RING)
    z_cat = jnp.concatenate(z_parts, axis=1)
    sizes = {a: lax.axis_size(a) for a in GENE_AXES}
    rings = {ROW_AXES: ROW_RING, COL_AXES: COL_RING}

    def member(coord, axes, back):
        ring = rings[axes]
        pos = ring.index(ravel([coord[a] for a in axes], [sizes[a] for a in axes]))
        out = dict(coord)
        out.update(zip(axes, unravel(ring[(pos - back) % len(ring)], [sizes[a] for a in axes])))
        return ravel([out[a] for a in GENE_AXES], [sizes[a] for a in GENE_AXES])

    def home(t1, t2, c):
        coord = dict(zip(GENE_AXES, unravel(c, [sizes[a] for a in GENE_AXES])))
        return member(coord, COL_AXES, t2) * gene_n + member(coord, ROW_AXES, t1)

    core = lax.axis_index("sc")
    ring_x = lax.axis_size("sx")
    pos_x = lax.axis_index("sx")
    every = SPOT_AXES + GENE_AXES
    received = []
    for phase in range(2):
        keep_lag = jnp.where(core == 0, lag_parts[2 * phase], lag_parts[2 * phase + 1])
        give_lag = jnp.where(core == 0, lag_parts[2 * phase + 1], lag_parts[2 * phase])
        keep = lax.dot_general(z_cat, keep_lag, contract_bins, preferred_element_type=jnp.float32)
        give = lax.dot_general(z_cat, give_lag, contract_bins, preferred_element_type=jnp.float32)
        mine = keep + lax.ppermute(give, "sc", [(0, 1), (1, 0)])
        total = lax.dynamic_slice_in_dim(mine, pos_x * panel_width, panel_width, 0)
        for d in range(1, ring_x):
            sent = lax.dynamic_slice_in_dim(mine, ((pos_x + d) % ring_x) * panel_width, panel_width, 0)
            total = total + lax.ppermute(sent, "sx", [(k, (k + d) % ring_x) for k in range(ring_x)])
        for high in range(2):
            perm = []
            for sx in range(ring_x):
                for sc in range(2):
                    sigma = (sx * 2 + high) * 2 + sc
                    for c in range(gene_n):
                        perm.append((sigma * gene_n + c, home(sx, sc + 2 * phase, c)))
            received.append(lax.ppermute(total, every, perm))
    share = received[0] + received[1] + received[2] + received[3]
    return share / jnp.sqrt(pair_norm)


def solution(mesh):
    spot_n, gene_n = mesh.devices.shape
    y_lo = 2 if gene_n >= 16 else 1
    z_a = gene_n // (y_lo * 2)
    split = jax.sharding.Mesh(
        mesh.devices.reshape(spot_n // 4, 2, 2, y_lo, z_a, 2), SPOT_AXES + GENE_AXES
    )
    gene = GENE_AXES
    placed = (P(SPOT_AXES, None, gene), P(SPOT_AXES, None), P(SPOT_AXES, None))
    return jax.shard_map(
        shards, mesh=split, in_specs=placed, out_specs=P(gene, SPOT_AXES), check_vma=False
    )
```

```python
import math

import jax
import jax.numpy as jnp
from jax import lax
from jax.sharding import PartitionSpec as P

stencil_taps = [
    (row_off, col_off, 1.0 / (row_off * row_off + col_off * col_off))
    for row_off in range(-2, 3)
    for col_off in range(-2, 3)
    if row_off != 0 or col_off != 0
]
contract_bins = (((0,), (0,)), ((), ()))
GENE_AXES = ("ylo", "za", "zv")
ROW_AXES = ("ylo", "zv")
COL_AXES = ("za",)
SPOT_AXES = ("sx", "syh", "sc")
ROW_RING = [0, 1, 3, 2]
COL_RING = [0, 1, 2, 3]


def padded(cells, sides, width):
    for axis, dim in sides:
        count = lax.axis_size(axis)
        ends = count - 1
        head = lax.slice_in_dim(cells, 0, width, axis=dim)
        tail = lax.slice_in_dim(cells, cells.shape[dim] - width, cells.shape[dim], axis=dim)
        cells = jnp.concatenate(
            [
                lax.ppermute(tail, axis, [(i, (i + 1) % count) for i in range(ends)]),
                cells,
                lax.ppermute(head, axis, [((i + 1) % count, i) for i in range(ends)]),
            ],
            axis=dim,
        )
    return cells


def allreduce_sum(vector, axes):
    count = math.prod(lax.axis_size(a) for a in axes)
    step = 1
    while step < count:
        vector = vector + lax.ppermute(vector, axes, [(i, i ^ step) for i in range(count)])
        step *= 2
    return vector


def centred_square_sum(n, s1, s2):
    base = 1 << 14
    s2_hi, s2_lo = s2 >> 14, s2 & (base - 1)
    s1_hi, s1_lo = s1 >> 14, s1 & (base - 1)
    c0 = n * s2_lo - s1_lo * s1_lo
    c1 = n * s2_hi - 2 * s1_hi * s1_lo + (c0 >> 14)
    c2 = -s1_hi * s1_hi + (c1 >> 14)
    upper = (c2 * base + (c1 & (base - 1))).astype(jnp.float32)
    return upper * base + (c0 & (base - 1)).astype(jnp.float32)


def ring_gather(block, axes, ring):
    size = len(ring)
    fwd = [(ring[k], ring[(k + 1) % size]) for k in range(size)]
    bwd = [(ring[(k + 1) % size], ring[k]) for k in range(size)]
    prev = lax.ppermute(block, axes, fwd)
    nxt = lax.ppermute(block, axes, bwd)
    half = block.shape[0] // 2
    far_lo = lax.ppermute(prev[:half], axes, fwd)
    far_hi = lax.ppermute(nxt[half:], axes, bwd)
    return [block, prev, jnp.concatenate([far_lo, far_hi], axis=0), nxt]


def unravel(index, sizes):
    out = []
    for size in reversed(sizes):
        index, rest = divmod(index, size)
        out.append(rest)
    return out[::-1]


def ravel(coords, sizes):
    index = 0
    for coord, size in zip(coords, sizes):
        index = index * size + coord
    return index


def shards(counts, tissue, tile_ids):
    row_count, col_count, panel_width = counts.shape
    spot_n = math.prod(lax.axis_size(a) for a in SPOT_AXES)
    gene_n = math.prod(lax.axis_size(a) for a in GENE_AXES)
    side = math.isqrt(gene_n)
    tile_code = tile_ids * 2 + tissue
    code_rims = padded(tile_code, ((SPOT_AXES, 0),), 2)
    code_wide = jnp.pad(code_rims, ((0, 0), (2, 2)))
    tissue_wide = code_wide % 2
    ids_wide = code_wide // 2
    weight_sq = jnp.zeros((row_count, col_count), jnp.int32)
    same_list = []
    for row_off, col_off, weight in stencil_taps:
        near_ids = ids_wide[
            2 + row_off : 2 + row_off + row_count, 2 + col_off : 2 + col_off + col_count
        ]
        near_tissue = tissue_wide[
            2 + row_off : 2 + row_off + row_count, 2 + col_off : 2 + col_off + col_count
        ]
        same = near_ids == tile_ids
        scaled = round(1600 * weight * weight)
        weight_sq = weight_sq + jnp.where(same, near_tissue * scaled, 0)
        same_list.append(same.astype(jnp.float32))
    in_tissue = tissue.astype(jnp.float32)
    mask = in_tissue[:, :, None]
    inside = jnp.where(tissue[:, :, None] > 0, counts, 0)
    local = jnp.concatenate(
        [
            jnp.sum(inside, axis=(0, 1)),
            jnp.sum(inside * inside, axis=(0, 1)),
            jnp.stack([jnp.sum(tissue), jnp.sum(tissue * weight_sq)]),
        ]
    )
    total = allreduce_sum(local, SPOT_AXES)
    count_int = total[2 * panel_width]
    tissue_count = count_int.astype(jnp.float32)
    pair_norm = total[2 * panel_width + 1].astype(jnp.float32) / 1600.0
    gene_mean = total[:panel_width].astype(jnp.float32) / tissue_count
    variance = (
        centred_square_sum(count_int, total[:panel_width], total[panel_width : 2 * panel_width])
        / tissue_count
        / tissue_count
    )
    values = counts.astype(jnp.float32)
    centred = (values - gene_mean) * mask
    zscores = (centred / jnp.sqrt(variance + 1e-05)).astype(jnp.bfloat16)
    zscore_rims = padded(zscores, ((SPOT_AXES, 0),), 2)
    zscore_wide = jnp.pad(zscore_rims, ((0, 0), (2, 2), (0, 0)))
    lagged_sum = jnp.zeros(values.shape, jnp.float32)
    for (row_off, col_off, weight), same_tile in zip(stencil_taps, same_list):
        near_z = zscore_wide[
            2 + row_off : 2 + row_off + row_count, 2 + col_off : 2 + col_off + col_count, :
        ]
        lagged_sum = lagged_sum + weight * same_tile[:, :, None] * near_z.astype(jnp.float32)
    lagged = lagged_sum.astype(jnp.bfloat16)
    bin_count = row_count * col_count
    flat_z = zscores.reshape(bin_count, panel_width)
    flat_lag = lagged.reshape(bin_count, panel_width)
    z_parts = ring_gather(flat_z, COL_AXES, COL_RING)
    lag_parts = ring_gather(flat_lag, ROW_AXES, ROW_RING)
    lag_cat = jnp.concatenate(lag_parts, axis=1)
    sizes = {a: lax.axis_size(a) for a in GENE_AXES}
    rings = {ROW_AXES: ROW_RING, COL_AXES: COL_RING}

    def member(coord, axes, back):
        ring = rings[axes]
        pos = ring.index(ravel([coord[a] for a in axes], [sizes[a] for a in axes]))
        out = dict(coord)
        out.update(zip(axes, unravel(ring[(pos - back) % len(ring)], [sizes[a] for a in axes])))
        return ravel([out[a] for a in GENE_AXES], [sizes[a] for a in GENE_AXES])

    def home(t1, t2, c):
        coord = dict(zip(GENE_AXES, unravel(c, [sizes[a] for a in GENE_AXES])))
        return member(coord, ROW_AXES, t2) * gene_n + member(coord, COL_AXES, t1)

    core = lax.axis_index("sc")
    ring_x = lax.axis_size("sx")
    pos_x = lax.axis_index("sx")
    every = SPOT_AXES + GENE_AXES
    received = []
    for phase in range(2):
        keep_z = jnp.where(core == 0, z_parts[2 * phase], z_parts[2 * phase + 1])
        give_z = jnp.where(core == 0, z_parts[2 * phase + 1], z_parts[2 * phase])
        keep = lax.dot_general(keep_z, lag_cat, contract_bins, preferred_element_type=jnp.float32)
        give = lax.dot_general(give_z, lag_cat, contract_bins, preferred_element_type=jnp.float32)
        mine = keep + lax.ppermute(give, "sc", [(0, 1), (1, 0)])
        total = lax.dynamic_slice_in_dim(mine, pos_x * panel_width, panel_width, 1)
        for d in range(1, ring_x):
            sent = lax.dynamic_slice_in_dim(mine, ((pos_x + d) % ring_x) * panel_width, panel_width, 1)
            total = total + lax.ppermute(sent, "sx", [(k, (k + d) % ring_x) for k in range(ring_x)])
        for high in range(2):
            perm = []
            for sx in range(ring_x):
                for sc in range(2):
                    sigma = (sx * 2 + high) * 2 + sc
                    for c in range(gene_n):
                        perm.append((sigma * gene_n + c, home(sc + 2 * phase, sx, c)))
            received.append(lax.ppermute(total, every, perm))
    share = received[0] + received[1] + received[2] + received[3]
    return share / jnp.sqrt(pair_norm)


def solution(mesh):
    spot_n, gene_n = mesh.devices.shape
    y_lo = 2 if gene_n >= 16 else 1
    z_a = gene_n // (y_lo * 2)
    split = jax.sharding.Mesh(
        mesh.devices.reshape(spot_n // 4, 2, 2, y_lo, z_a, 2), SPOT_AXES + GENE_AXES
    )
    gene = GENE_AXES
    placed = (P(SPOT_AXES, None, gene), P(SPOT_AXES, None), P(SPOT_AXES, None))
    return jax.shard_map(
        shards, mesh=split, in_specs=placed, out_specs=P(gene, SPOT_AXES), check_vma=False
    )
```

```python
import math

import jax
import jax.numpy as jnp
from jax import lax
from jax.sharding import PartitionSpec as P

stencil_taps = [
    (row_off, col_off, 1.0 / (row_off * row_off + col_off * col_off))
    for row_off in range(-2, 3)
    for col_off in range(-2, 3)
    if row_off != 0 or col_off != 0
]
contract_bins = (((0,), (0,)), ((), ()))
GENE_AXES = ("ylo", "za", "zv")
ROW_AXES = ("ylo", "zv")
COL_AXES = ("za",)
SPOT_AXES = ("sx", "syh", "sc")
ROW_RING = [0, 1, 3, 2]
COL_RING = [0, 1, 2, 3]


def padded(cells, sides, width):
    for axis, dim in sides:
        count = lax.axis_size(axis)
        ends = count - 1
        head = lax.slice_in_dim(cells, 0, width, axis=dim)
        tail = lax.slice_in_dim(cells, cells.shape[dim] - width, cells.shape[dim], axis=dim)
        cells = jnp.concatenate(
            [
                lax.ppermute(tail, axis, [(i, (i + 1) % count) for i in range(ends)]),
                cells,
                lax.ppermute(head, axis, [((i + 1) % count, i) for i in range(ends)]),
            ],
            axis=dim,
        )
    return cells


def allreduce_sum(vector, axes):
    count = math.prod(lax.axis_size(a) for a in axes)
    step = 1
    while step < count:
        vector = vector + lax.ppermute(vector, axes, [(i, i ^ step) for i in range(count)])
        step *= 2
    return vector


def centred_square_sum(n, s1, s2):
    base = 1 << 14
    s2_hi, s2_lo = s2 >> 14, s2 & (base - 1)
    s1_hi, s1_lo = s1 >> 14, s1 & (base - 1)
    c0 = n * s2_lo - s1_lo * s1_lo
    c1 = n * s2_hi - 2 * s1_hi * s1_lo + (c0 >> 14)
    c2 = -s1_hi * s1_hi + (c1 >> 14)
    upper = (c2 * base + (c1 & (base - 1))).astype(jnp.float32)
    return upper * base + (c0 & (base - 1)).astype(jnp.float32)


def ring_shift(block, axes, ring):
    size = len(ring)
    out = [block]
    for t in range(1, size):
        out.append(lax.ppermute(block, axes, [(ring[k], ring[(k + t) % size]) for k in range(size)]))
    return out


def ring_gather(block, axes, ring):
    size = len(ring)
    fwd = [(ring[k], ring[(k + 1) % size]) for k in range(size)]
    bwd = [(ring[(k + 1) % size], ring[k]) for k in range(size)]
    prev = lax.ppermute(block, axes, fwd)
    nxt = lax.ppermute(block, axes, bwd)
    half = block.shape[0] // 2
    far_lo = lax.ppermute(prev[:half], axes, fwd)
    far_hi = lax.ppermute(nxt[half:], axes, bwd)
    return [block, prev, jnp.concatenate([far_lo, far_hi], axis=0), nxt]


def unravel(index, sizes):
    out = []
    for size in reversed(sizes):
        index, rest = divmod(index, size)
        out.append(rest)
    return out[::-1]


def ravel(coords, sizes):
    index = 0
    for coord, size in zip(coords, sizes):
        index = index * size + coord
    return index


def shards(counts, tissue, tile_ids):
    row_count, col_count, panel_width = counts.shape
    spot_n = math.prod(lax.axis_size(a) for a in SPOT_AXES)
    gene_n = math.prod(lax.axis_size(a) for a in GENE_AXES)
    side = math.isqrt(gene_n)
    tile_code = tile_ids * 2 + tissue
    code_rims = padded(tile_code, ((SPOT_AXES, 0),), 2)
    code_wide = jnp.pad(code_rims, ((0, 0), (2, 2)))
    tissue_wide = code_wide % 2
    ids_wide = code_wide // 2
    weight_sq = jnp.zeros((row_count, col_count), jnp.int32)
    same_list = []
    for row_off, col_off, weight in stencil_taps:
        near_ids = ids_wide[
            2 + row_off : 2 + row_off + row_count, 2 + col_off : 2 + col_off + col_count
        ]
        near_tissue = tissue_wide[
            2 + row_off : 2 + row_off + row_count, 2 + col_off : 2 + col_off + col_count
        ]
        same = near_ids == tile_ids
        scaled = round(1600 * weight * weight)
        weight_sq = weight_sq + jnp.where(same, near_tissue * scaled, 0)
        same_list.append(same.astype(jnp.float32))
    in_tissue = tissue.astype(jnp.float32)
    mask = in_tissue[:, :, None]
    inside = jnp.where(tissue[:, :, None] > 0, counts, 0)
    local = jnp.concatenate(
        [
            jnp.sum(inside, axis=(0, 1)),
            jnp.sum(inside * inside, axis=(0, 1)),
            jnp.stack([jnp.sum(tissue), jnp.sum(tissue * weight_sq)]),
        ]
    )
    total = allreduce_sum(local, SPOT_AXES)
    count_int = total[2 * panel_width]
    tissue_count = count_int.astype(jnp.float32)
    pair_norm = total[2 * panel_width + 1].astype(jnp.float32) / 1600.0
    gene_mean = total[:panel_width].astype(jnp.float32) / tissue_count
    variance = (
        centred_square_sum(count_int, total[:panel_width], total[panel_width : 2 * panel_width])
        / tissue_count
        / tissue_count
    )
    values = counts.astype(jnp.float32)
    centred = (values - gene_mean) * mask
    zscores = (centred / jnp.sqrt(variance + 1e-05)).astype(jnp.bfloat16)
    zscore_rims = padded(zscores, ((SPOT_AXES, 0),), 2)
    zscore_wide = jnp.pad(zscore_rims, ((0, 0), (2, 2), (0, 0)))
    lagged_sum = jnp.zeros(values.shape, jnp.float32)
    for (row_off, col_off, weight), same_tile in zip(stencil_taps, same_list):
        near_z = zscore_wide[
            2 + row_off : 2 + row_off + row_count, 2 + col_off : 2 + col_off + col_count, :
        ]
        lagged_sum = lagged_sum + weight * same_tile[:, :, None] * near_z.astype(jnp.float32)
    lagged = lagged_sum.astype(jnp.bfloat16)
    bin_count = row_count * col_count
    flat_z = zscores.reshape(bin_count, panel_width)
    flat_lag = lagged.reshape(bin_count, panel_width)
    z_parts = ring_shift(flat_z, ROW_AXES, ROW_RING)
    lag_parts = ring_gather(flat_lag, COL_AXES, COL_RING)
    z_cat = jnp.concatenate(z_parts, axis=1)
    sizes = {a: lax.axis_size(a) for a in GENE_AXES}
    rings = {ROW_AXES: ROW_RING, COL_AXES: COL_RING}

    def member(coord, axes, back):
        ring = rings[axes]
        pos = ring.index(ravel([coord[a] for a in axes], [sizes[a] for a in axes]))
        out = dict(coord)
        out.update(zip(axes, unravel(ring[(pos - back) % len(ring)], [sizes[a] for a in axes])))
        return ravel([out[a] for a in GENE_AXES], [sizes[a] for a in GENE_AXES])

    def home(t1, t2, c):
        coord = dict(zip(GENE_AXES, unravel(c, [sizes[a] for a in GENE_AXES])))
        return member(coord, COL_AXES, t2) * gene_n + member(coord, ROW_AXES, t1)

    core = lax.axis_index("sc")
    ring_x = lax.axis_size("sx")
    pos_x = lax.axis_index("sx")
    every = SPOT_AXES + GENE_AXES
    received = []
    for phase in range(2):
        keep_lag = jnp.where(core == 0, lag_parts[2 * phase], lag_parts[2 * phase + 1])
        give_lag = jnp.where(core == 0, lag_parts[2 * phase + 1], lag_parts[2 * phase])
        keep = lax.dot_general(z_cat, keep_lag, contract_bins, preferred_element_type=jnp.float32)
        give = lax.dot_general(z_cat, give_lag, contract_bins, preferred_element_type=jnp.float32)
        mine = keep + lax.ppermute(give, "sc", [(0, 1), (1, 0)])
        total = lax.dynamic_slice_in_dim(mine, pos_x * panel_width, panel_width, 0)
        for d in range(1, ring_x):
            sent = lax.dynamic_slice_in_dim(mine, ((pos_x + d) % ring_x) * panel_width, panel_width, 0)
            total = total + lax.ppermute(sent, "sx", [(k, (k + d) % ring_x) for k in range(ring_x)])
        for high in range(2):
            perm = []
            for sx in range(ring_x):
                for sc in range(2):
                    sigma = (sx * 2 + high) * 2 + sc
                    for c in range(gene_n):
                        perm.append((sigma * gene_n + c, home(sx, sc + 2 * phase, c)))
            received.append(lax.ppermute(total, every, perm))
    share = received[0] + received[1] + received[2] + received[3]
    return share / jnp.sqrt(pair_norm)


def solution(mesh):
    spot_n, gene_n = mesh.devices.shape
    y_lo = 2 if gene_n >= 16 else 1
    z_a = gene_n // (y_lo * 2)
    split = jax.sharding.Mesh(
        mesh.devices.reshape(spot_n // 4, 2, 2, y_lo, z_a, 2), SPOT_AXES + GENE_AXES
    )
    gene = GENE_AXES
    placed = (P(SPOT_AXES, None, gene), P(SPOT_AXES, None), P(SPOT_AXES, None))
    return jax.shard_map(
        shards, mesh=split, in_specs=placed, out_specs=P(gene, SPOT_AXES), check_vma=False
    )
```

```python
import math

import jax
import jax.numpy as jnp
from jax import lax
from jax.sharding import PartitionSpec as P

stencil_taps = [
    (row_off, col_off, 1.0 / (row_off * row_off + col_off * col_off))
    for row_off in range(-2, 3)
    for col_off in range(-2, 3)
    if row_off != 0 or col_off != 0
]
contract_bins = (((0,), (0,)), ((), ()))
GENE_AXES = ("ylo", "za", "zv")
ROW_AXES = ("ylo", "zv")
COL_AXES = ("za",)
SPOT_AXES = ("sx", "syh", "sc")
ROW_RING = [0, 1, 3, 2]
COL_RING = [0, 1, 2, 3]


def padded(cells, sides, width):
    for axis, dim in sides:
        count = lax.axis_size(axis)
        ends = count - 1
        head = lax.slice_in_dim(cells, 0, width, axis=dim)
        tail = lax.slice_in_dim(cells, cells.shape[dim] - width, cells.shape[dim], axis=dim)
        cells = jnp.concatenate(
            [
                lax.ppermute(tail, axis, [(i, (i + 1) % count) for i in range(ends)]),
                cells,
                lax.ppermute(head, axis, [((i + 1) % count, i) for i in range(ends)]),
            ],
            axis=dim,
        )
    return cells


def allreduce_sum(vector, axes):
    count = math.prod(lax.axis_size(a) for a in axes)
    step = 1
    while step < count:
        vector = vector + lax.ppermute(vector, axes, [(i, i ^ step) for i in range(count)])
        step *= 2
    return vector


def centred_square_sum(n, s1, s2):
    base = 1 << 14
    s2_hi, s2_lo = s2 >> 14, s2 & (base - 1)
    s1_hi, s1_lo = s1 >> 14, s1 & (base - 1)
    c0 = n * s2_lo - s1_lo * s1_lo
    c1 = n * s2_hi - 2 * s1_hi * s1_lo + (c0 >> 14)
    c2 = -s1_hi * s1_hi + (c1 >> 14)
    upper = (c2 * base + (c1 & (base - 1))).astype(jnp.float32)
    return upper * base + (c0 & (base - 1)).astype(jnp.float32)


def ring_gather(block, axes, ring):
    size = len(ring)
    fwd = [(ring[k], ring[(k + 1) % size]) for k in range(size)]
    bwd = [(ring[(k + 1) % size], ring[k]) for k in range(size)]
    prev = lax.ppermute(block, axes, fwd)
    nxt = lax.ppermute(block, axes, bwd)
    half = block.shape[0] // 2
    far_lo = lax.ppermute(prev[:half], axes, fwd)
    far_hi = lax.ppermute(nxt[half:], axes, bwd)
    return [block, prev, (far_lo, far_hi), nxt]


def unravel(index, sizes):
    out = []
    for size in reversed(sizes):
        index, rest = divmod(index, size)
        out.append(rest)
    return out[::-1]


def ravel(coords, sizes):
    index = 0
    for coord, size in zip(coords, sizes):
        index = index * size + coord
    return index


def shards(counts, tissue, tile_ids):
    row_count, col_count, panel_width = counts.shape
    spot_n = math.prod(lax.axis_size(a) for a in SPOT_AXES)
    gene_n = math.prod(lax.axis_size(a) for a in GENE_AXES)
    side = math.isqrt(gene_n)
    tile_code = tile_ids * 2 + tissue
    code_rims = padded(tile_code, ((SPOT_AXES, 0),), 2)
    code_wide = jnp.pad(code_rims, ((0, 0), (2, 2)))
    tissue_wide = code_wide % 2
    ids_wide = code_wide // 2
    weight_sq = jnp.zeros((row_count, col_count), jnp.int32)
    same_list = []
    for row_off, col_off, weight in stencil_taps:
        near_ids = ids_wide[
            2 + row_off : 2 + row_off + row_count, 2 + col_off : 2 + col_off + col_count
        ]
        near_tissue = tissue_wide[
            2 + row_off : 2 + row_off + row_count, 2 + col_off : 2 + col_off + col_count
        ]
        same = near_ids == tile_ids
        scaled = round(1600 * weight * weight)
        weight_sq = weight_sq + jnp.where(same, near_tissue * scaled, 0)
        same_list.append(same.astype(jnp.float32))
    in_tissue = tissue.astype(jnp.float32)
    mask = in_tissue[:, :, None]
    inside = jnp.where(tissue[:, :, None] > 0, counts, 0)
    local = jnp.concatenate(
        [
            jnp.sum(inside, axis=(0, 1)),
            jnp.sum(inside * inside, axis=(0, 1)),
            jnp.stack([jnp.sum(tissue), jnp.sum(tissue * weight_sq)]),
        ]
    )
    total = allreduce_sum(local, SPOT_AXES)
    count_int = total[2 * panel_width]
    tissue_count = count_int.astype(jnp.float32)
    pair_norm = total[2 * panel_width + 1].astype(jnp.float32) / 1600.0
    gene_mean = total[:panel_width].astype(jnp.float32) / tissue_count
    variance = (
        centred_square_sum(count_int, total[:panel_width], total[panel_width : 2 * panel_width])
        / tissue_count
        / tissue_count
    )
    values = counts.astype(jnp.float32)
    centred = (values - gene_mean) * mask
    zscores = (centred / jnp.sqrt(variance + 1e-05)).astype(jnp.bfloat16)
    zscore_rims = padded(zscores, ((SPOT_AXES, 0),), 2)
    zscore_wide = jnp.pad(zscore_rims, ((0, 0), (2, 2), (0, 0)))
    lagged_sum = jnp.zeros(values.shape, jnp.float32)
    for (row_off, col_off, weight), same_tile in zip(stencil_taps, same_list):
        near_z = zscore_wide[
            2 + row_off : 2 + row_off + row_count, 2 + col_off : 2 + col_off + col_count, :
        ]
        lagged_sum = lagged_sum + weight * same_tile[:, :, None] * near_z.astype(jnp.float32)
    lagged = lagged_sum.astype(jnp.bfloat16)
    bin_count = row_count * col_count
    flat_z = zscores.reshape(bin_count, panel_width)
    flat_lag = lagged.reshape(bin_count, panel_width)
    z_parts = ring_gather(flat_z, ROW_AXES, ROW_RING)
    z_parts[2] = jnp.concatenate(z_parts[2], axis=0)
    lag_parts = ring_gather(flat_lag, COL_AXES, COL_RING)
    z_cat = jnp.concatenate(z_parts, axis=1)
    half_bins = bin_count // 2
    lag_halves = [
        part if isinstance(part, tuple) else (part[:half_bins], part[half_bins:]) for part in lag_parts
    ]
    z_halves = (z_cat[:half_bins], z_cat[half_bins:])

    def product(pick):
        return sum(
            lax.dot_general(z_halves[h], pick(h), contract_bins, preferred_element_type=jnp.float32)
            for h in range(2)
        )
    sizes = {a: lax.axis_size(a) for a in GENE_AXES}
    rings = {ROW_AXES: ROW_RING, COL_AXES: COL_RING}

    def member(coord, axes, back):
        ring = rings[axes]
        pos = ring.index(ravel([coord[a] for a in axes], [sizes[a] for a in axes]))
        out = dict(coord)
        out.update(zip(axes, unravel(ring[(pos - back) % len(ring)], [sizes[a] for a in axes])))
        return ravel([out[a] for a in GENE_AXES], [sizes[a] for a in GENE_AXES])

    def home(t1, t2, c):
        coord = dict(zip(GENE_AXES, unravel(c, [sizes[a] for a in GENE_AXES])))
        return member(coord, COL_AXES, t2) * gene_n + member(coord, ROW_AXES, t1)

    core = lax.axis_index("sc")
    ring_x = lax.axis_size("sx")
    pos_x = lax.axis_index("sx")
    every = SPOT_AXES + GENE_AXES
    received = []
    for phase in range(2):
        first, second = lag_halves[2 * phase], lag_halves[2 * phase + 1]
        keep = product(lambda h: jnp.where(core == 0, first[h], second[h]))
        give = product(lambda h: jnp.where(core == 0, second[h], first[h]))
        mine = keep + lax.ppermute(give, "sc", [(0, 1), (1, 0)])
        total = lax.dynamic_slice_in_dim(mine, pos_x * panel_width, panel_width, 0)
        for d in range(1, ring_x):
            sent = lax.dynamic_slice_in_dim(mine, ((pos_x + d) % ring_x) * panel_width, panel_width, 0)
            total = total + lax.ppermute(sent, "sx", [(k, (k + d) % ring_x) for k in range(ring_x)])
        for high in range(2):
            perm = []
            for sx in range(ring_x):
                for sc in range(2):
                    sigma = (sx * 2 + high) * 2 + sc
                    for c in range(gene_n):
                        perm.append((sigma * gene_n + c, home(sx, sc + 2 * phase, c)))
            received.append(lax.ppermute(total, every, perm))
    share = received[0] + received[1] + received[2] + received[3]
    return share / jnp.sqrt(pair_norm)


def solution(mesh):
    spot_n, gene_n = mesh.devices.shape
    y_lo = 2 if gene_n >= 16 else 1
    z_a = gene_n // (y_lo * 2)
    split = jax.sharding.Mesh(
        mesh.devices.reshape(spot_n // 4, 2, 2, y_lo, z_a, 2), SPOT_AXES + GENE_AXES
    )
    gene = GENE_AXES
    placed = (P(SPOT_AXES, None, gene), P(SPOT_AXES, None), P(SPOT_AXES, None))
    return jax.shard_map(
        shards, mesh=split, in_specs=placed, out_specs=P(gene, SPOT_AXES), check_vma=False
    )
```

```python
import math

import jax
import jax.numpy as jnp
from jax import lax
from jax.sharding import PartitionSpec as P

stencil_taps = [
    (row_off, col_off, 1.0 / (row_off * row_off + col_off * col_off))
    for row_off in range(-2, 3)
    for col_off in range(-2, 3)
    if row_off != 0 or col_off != 0
]
contract_bins = (((0,), (0,)), ((), ()))
GENE_AXES = ("ylo", "za", "zv")
ROW_AXES = ("ylo", "zv")
COL_AXES = ("za",)
SPOT_AXES = ("sx", "syh", "sc")
ROW_RING = [0, 1, 3, 2]
COL_RING = [0, 1, 2, 3]


def padded(cells, sides, width):
    for axis, dim in sides:
        count = lax.axis_size(axis)
        ends = count - 1
        head = lax.slice_in_dim(cells, 0, width, axis=dim)
        tail = lax.slice_in_dim(cells, cells.shape[dim] - width, cells.shape[dim], axis=dim)
        cells = jnp.concatenate(
            [
                lax.ppermute(tail, axis, [(i, (i + 1) % count) for i in range(ends)]),
                cells,
                lax.ppermute(head, axis, [((i + 1) % count, i) for i in range(ends)]),
            ],
            axis=dim,
        )
    return cells


def allreduce_sum(vector, axes):
    count = math.prod(lax.axis_size(a) for a in axes)
    step = 1
    while step < count:
        vector = vector + lax.ppermute(vector, axes, [(i, i ^ step) for i in range(count)])
        step *= 2
    return vector


def centred_square_sum(n, s1, s2):
    base = 1 << 14
    s2_hi, s2_lo = s2 >> 14, s2 & (base - 1)
    s1_hi, s1_lo = s1 >> 14, s1 & (base - 1)
    c0 = n * s2_lo - s1_lo * s1_lo
    c1 = n * s2_hi - 2 * s1_hi * s1_lo + (c0 >> 14)
    c2 = -s1_hi * s1_hi + (c1 >> 14)
    upper = (c2 * base + (c1 & (base - 1))).astype(jnp.float32)
    return upper * base + (c0 & (base - 1)).astype(jnp.float32)


def ring_gather(block, axes, ring):
    size = len(ring)
    fwd = [(ring[k], ring[(k + 1) % size]) for k in range(size)]
    bwd = [(ring[(k + 1) % size], ring[k]) for k in range(size)]
    prev = lax.ppermute(block, axes, fwd)
    nxt = lax.ppermute(block, axes, bwd)
    half = block.shape[0] // 2
    far_lo = lax.ppermute(prev[:half], axes, fwd)
    far_hi = lax.ppermute(nxt[half:], axes, bwd)
    return [block, prev, jnp.concatenate([far_lo, far_hi], axis=0), nxt]


def unravel(index, sizes):
    out = []
    for size in reversed(sizes):
        index, rest = divmod(index, size)
        out.append(rest)
    return out[::-1]


def ravel(coords, sizes):
    index = 0
    for coord, size in zip(coords, sizes):
        index = index * size + coord
    return index


def shards(counts, tissue, tile_ids):
    row_count, col_count, panel_width = counts.shape
    spot_n = math.prod(lax.axis_size(a) for a in SPOT_AXES)
    gene_n = math.prod(lax.axis_size(a) for a in GENE_AXES)
    side = math.isqrt(gene_n)
    tile_code = tile_ids * 2 + tissue
    code_rims = padded(tile_code, ((SPOT_AXES, 0),), 2)
    code_wide = jnp.pad(code_rims, ((0, 0), (2, 2)))
    tissue_wide = code_wide % 2
    ids_wide = code_wide // 2
    weight_sq = jnp.zeros((row_count, col_count), jnp.int32)
    same_list = []
    for row_off, col_off, weight in stencil_taps:
        near_ids = ids_wide[
            2 + row_off : 2 + row_off + row_count, 2 + col_off : 2 + col_off + col_count
        ]
        near_tissue = tissue_wide[
            2 + row_off : 2 + row_off + row_count, 2 + col_off : 2 + col_off + col_count
        ]
        same = near_ids == tile_ids
        scaled = round(1600 * weight * weight)
        weight_sq = weight_sq + jnp.where(same, near_tissue * scaled, 0)
        same_list.append(same.astype(jnp.float32))
    in_tissue = tissue.astype(jnp.float32)
    mask = in_tissue[:, :, None]
    inside = jnp.where(tissue[:, :, None] > 0, counts, 0)
    local = jnp.concatenate(
        [
            jnp.sum(inside, axis=(0, 1)),
            jnp.sum(inside * inside, axis=(0, 1)),
            jnp.sum(tissue)[None],
        ]
    )
    total = allreduce_sum(local, SPOT_AXES)
    count_int = total[2 * panel_width]
    tissue_count = count_int.astype(jnp.float32)
    pair_int = allreduce_sum(jnp.sum(tissue * weight_sq)[None], SPOT_AXES)
    pair_norm = pair_int[0].astype(jnp.float32) / 1600.0
    gene_mean = total[:panel_width].astype(jnp.float32) / tissue_count
    variance = (
        centred_square_sum(count_int, total[:panel_width], total[panel_width : 2 * panel_width])
        / tissue_count
        / tissue_count
    )
    values = counts.astype(jnp.float32)
    centred = (values - gene_mean) * mask
    zscores = (centred / jnp.sqrt(variance + 1e-05)).astype(jnp.bfloat16)
    zscore_rims = padded(zscores, ((SPOT_AXES, 0),), 2)
    zscore_wide = jnp.pad(zscore_rims, ((0, 0), (2, 2), (0, 0)))
    lagged_sum = jnp.zeros(values.shape, jnp.float32)
    for (row_off, col_off, weight), same_tile in zip(stencil_taps, same_list):
        near_z = zscore_wide[
            2 + row_off : 2 + row_off + row_count, 2 + col_off : 2 + col_off + col_count, :
        ]
        lagged_sum = lagged_sum + weight * same_tile[:, :, None] * near_z.astype(jnp.float32)
    lagged = lagged_sum.astype(jnp.bfloat16)
    bin_count = row_count * col_count
    flat_z = zscores.reshape(bin_count, panel_width)
    flat_lag = lagged.reshape(bin_count, panel_width)
    z_parts = ring_gather(flat_z, ROW_AXES, ROW_RING)
    lag_parts = ring_gather(flat_lag, COL_AXES, COL_RING)
    z_cat = jnp.concatenate(z_parts, axis=1)
    sizes = {a: lax.axis_size(a) for a in GENE_AXES}
    rings = {ROW_AXES: ROW_RING, COL_AXES: COL_RING}

    def member(coord, axes, back):
        ring = rings[axes]
        pos = ring.index(ravel([coord[a] for a in axes], [sizes[a] for a in axes]))
        out = dict(coord)
        out.update(zip(axes, unravel(ring[(pos - back) % len(ring)], [sizes[a] for a in axes])))
        return ravel([out[a] for a in GENE_AXES], [sizes[a] for a in GENE_AXES])

    def home(t1, t2, c):
        coord = dict(zip(GENE_AXES, unravel(c, [sizes[a] for a in GENE_AXES])))
        return member(coord, COL_AXES, t2) * gene_n + member(coord, ROW_AXES, t1)

    core = lax.axis_index("sc")
    ring_x = lax.axis_size("sx")
    pos_x = lax.axis_index("sx")
    every = SPOT_AXES + GENE_AXES
    received = []
    for phase in range(2):
        keep_lag = jnp.where(core == 0, lag_parts[2 * phase], lag_parts[2 * phase + 1])
        give_lag = jnp.where(core == 0, lag_parts[2 * phase + 1], lag_parts[2 * phase])
        keep = lax.dot_general(z_cat, keep_lag, contract_bins, preferred_element_type=jnp.float32)
        give = lax.dot_general(z_cat, give_lag, contract_bins, preferred_element_type=jnp.float32)
        mine = keep + lax.ppermute(give, "sc", [(0, 1), (1, 0)])
        total = lax.dynamic_slice_in_dim(mine, pos_x * panel_width, panel_width, 0)
        for d in range(1, ring_x):
            sent = lax.dynamic_slice_in_dim(mine, ((pos_x + d) % ring_x) * panel_width, panel_width, 0)
            total = total + lax.ppermute(sent, "sx", [(k, (k + d) % ring_x) for k in range(ring_x)])
        for high in range(2):
            perm = []
            for sx in range(ring_x):
                for sc in range(2):
                    sigma = (sx * 2 + high) * 2 + sc
                    for c in range(gene_n):
                        perm.append((sigma * gene_n + c, home(sx, sc + 2 * phase, c)))
            received.append(lax.ppermute(total, every, perm))
    share = received[0] + received[1] + received[2] + received[3]
    return share / jnp.sqrt(pair_norm)


def solution(mesh):
    spot_n, gene_n = mesh.devices.shape
    y_lo = 2 if gene_n >= 16 else 1
    z_a = gene_n // (y_lo * 2)
    split = jax.sharding.Mesh(
        mesh.devices.reshape(spot_n // 4, 2, 2, y_lo, z_a, 2), SPOT_AXES + GENE_AXES
    )
    gene = GENE_AXES
    placed = (P(SPOT_AXES, None, gene), P(SPOT_AXES, None), P(SPOT_AXES, None))
    return jax.shard_map(
        shards, mesh=split, in_specs=placed, out_specs=P(gene, SPOT_AXES), check_vma=False
    )
```
